512 devices in a mesh: seq: 32 (over x, y), row: 4 (over z_hi, core), col: 4 (over z_lo).
Axes of the slice: x: 4, y: 8, z: 8 (z_hi: 2, z_lo: 4; z = z_hi * 4 + z_lo), core: 2. Of those that a mesh axis runs over, the one named last changes fastest.
Arguments:
- queries: bfloat16 [2048, 8192], P(('seq', 'row', 'col')), may hold values from -6 to 6
- new_keys: bfloat16 [2048, 1024], P(('seq', 'row', 'col')), may hold values from -6 to 6
- new_values: bfloat16 [2048, 1024], P(('seq', 'row', 'col')), may hold values from -6 to 6
- positions: int32 [2048], P(('seq', 'row', 'col')), may hold values from 0 to 2047, each once
- cache_keys: bfloat16 [4096, 1024], P(('row', 'col')), may hold values from -6 to 6
- cache_values: bfloat16 [4096, 1024], P(('row', 'col')), may hold values from -6 to 6
- slab_start: int32 [1], replicated, may hold values from 2048 to 4096
Outputs:
- context: bfloat16 [2048, 8192], P(('seq', 'row', 'col'))
The draws below stay inside these ranges and needn't reach their ends.
Inputs may be any that keep to these rules, and one draw needn't show every extreme that they name: positions holds every number of 0 to 2047 once.
All inputs are finite; a program needn't handle non-finite values.
Results may differ from the reference program's by a relative error of at most 0.0065.
Values may be sent and summed in bfloat16 or wider, within the bound.
No kernel may reach another device: no remote copies, remote signals or barrier semaphores. Data moves between devices by JAX's collectives and lax.ppermute only.
A program may use at most 64 MiB of HBM per device.

```python
import math
import jax
import jax.numpy as jnp
from jax import lax

HQ = 64
KVH = 8
HD = 128
PREFIX = 4096
TOKENS = 2048


def draw_queries(key, part):
    array_shape = (TOKENS, HQ * HD)
    noise_key = jax.random.fold_in(key, 3)
    values = jnp.clip(jax.random.normal(noise_key, array_shape, jnp.float32), -6.0, 6.0)
    return values.astype(jnp.bfloat16)


def draw_cache_keys(key, part):
    array_shape = (PREFIX, KVH * HD)
    noise_key = jax.random.fold_in(key, 5)
    values = jnp.clip(jax.random.normal(noise_key, array_shape, jnp.float32), -6.0, 6.0)
    return values.astype(jnp.bfloat16)


def levels(key, extent, shards, least, top_value):
    factor_of, own = 1.0, jax.random.fold_in(key, 6)
    for dim, shards_of in shards:
        heights = jnp.exp(jax.random.uniform(jax.random.fold_in(own, dim), (shards_of,), jnp.float32, least / len(shards), top_value / len(shards)))
        factor_of = factor_of * jnp.repeat(heights, extent[dim] // shards_of).reshape([-1 if axis == dim else 1 for axis in range(len(extent))])
    return factor_of


def noise(rng, shape, deviation, most, split=(), held_as=jnp.bfloat16):
    gain = levels(rng, shape, split, -0.22, 0.18) if split else 1.0
    drawn = jax.random.normal(rng, shape, jnp.float32) * deviation * gain
    return jnp.minimum(jnp.maximum(drawn, -most), most).astype(held_as)


def setup_inputs(seed: int = 0) -> dict:
    arg_keys = jax.random.split(jax.random.key(seed), 8)
    queries = draw_queries(jax.random.fold_in(arg_keys[7], 71), 0)
    new_keys = noise(arg_keys[1], (TOKENS, KVH * HD), 1.0, 6.0, ((0, 512),))
    new_values = noise(arg_keys[2], (TOKENS, KVH * HD), 1.0, 6.0, ((0, 512),))
    positions = jax.random.permutation(arg_keys[3], TOKENS).astype(jnp.int32)
    cache_keys = draw_cache_keys(jax.random.fold_in(arg_keys[7], 71), 0)
    cache_values = noise(arg_keys[5], (PREFIX, KVH * HD), 1.0, 6.0, ((0, 16),))
    slab_start = jax.random.randint(arg_keys[6], (1,), PREFIX // 2, PREFIX + 1).astype(jnp.int32)
    return {"queries": queries, "new_keys": new_keys, "new_values": new_values, "positions": positions, "cache_keys": cache_keys, "cache_values": cache_values, "slab_start": slab_start}


far_position = 1073741824

def reference(queries, new_keys, new_values, positions, cache_keys, cache_values, slab_start):
    first_pos = slab_start[0]
    query_pos = (first_pos + positions).astype(jnp.int32)
    cache_index = jnp.arange(PREFIX, dtype=jnp.int32)
    cache_pos = jnp.where(cache_index < first_pos, cache_index, jnp.int32(far_position)).astype(jnp.int32)
    key_pos = jnp.concatenate([cache_pos, query_pos]).astype(jnp.int32)
    all_keys = jnp.concatenate([cache_keys, new_keys], 0).reshape(PREFIX + TOKENS, KVH, HD)
    all_values = jnp.concatenate([cache_values, new_values], 0).reshape(PREFIX + TOKENS, KVH, HD)
    allowed = key_pos[None, :] <= query_pos[:, None]
    head_queries = queries.reshape(TOKENS, HQ, HD).transpose(1, 0, 2)
    group_size = HQ // KVH
    score_scale = 1.0 / math.sqrt(HD)

    def one_head(inputs):
        head_index, query_head = inputs
        kv_index = head_index // group_size
        head_keys = lax.dynamic_index_in_dim(all_keys, kv_index, 1, keepdims=False)
        head_values = lax.dynamic_index_in_dim(all_values, kv_index, 1, keepdims=False)
        scores = jnp.dot(query_head, head_keys.T, preferred_element_type=jnp.float32) * score_scale
        row_max = lax.optimization_barrier(jnp.max(jnp.where(allowed, scores, -jnp.inf), axis=1, keepdims=True))
        exponent = jnp.where(allowed, jnp.exp(scores - row_max), 0.0)
        denominator = lax.optimization_barrier(jnp.sum(exponent, axis=1, keepdims=True))
        weights = exponent.astype(jnp.bfloat16)
        summed = jnp.dot(weights, head_values, preferred_element_type=jnp.float32)
        return (summed / denominator).astype(jnp.bfloat16)
    context = lax.map(one_head, (jnp.arange(HQ, dtype=jnp.int32), head_queries))
    return context.transpose(1, 0, 2).reshape(TOKENS, HQ * HD)
```

```python
import math

import numpy as np
import jax
import jax.numpy as jnp
from jax import lax
from jax.sharding import PartitionSpec as P

HQ = 64
KVH = 8
HD = 128

far_position = 1073741824
code_base = 256


def gather_cells(block, cell_axes, cell_count):
    spread = jnp.broadcast_to(block[None], (cell_count,) + block.shape)
    return lax.all_to_all(spread, cell_axes, 0, 0, tiled=True)


def on_device(queries, new_keys, new_values, positions, cache_keys, cache_values, slab_start):
    seq_count = lax.axis_size("seq")
    cell_axes = ("row", "col")
    cell_count = lax.axis_size("row") * lax.axis_size("col")
    heads_dev = HQ // seq_count
    group_size = HQ // KVH
    tok_rows = queries.shape[0]
    first_pos = slab_start[0]

    kv_of_peer = np.arange(seq_count) * heads_dev // group_size
    kv_first = lax.axis_index("seq") * heads_dev // group_size

    q_part = queries.reshape(tok_rows, seq_count, heads_dev * HD).transpose(1, 0, 2)
    k_part = jnp.take(new_keys.reshape(tok_rows, KVH, HD), kv_of_peer, axis=1).transpose(1, 0, 2)
    v_part = jnp.take(new_values.reshape(tok_rows, KVH, HD), kv_of_peer, axis=1).transpose(1, 0, 2)
    codes = jnp.stack([positions // code_base, positions % code_base], axis=1).astype(jnp.bfloat16)
    codes = jnp.pad(codes.reshape(1, tok_rows * 2), ((0, 0), (0, 128 - tok_rows * 2)))
    send = jnp.concatenate(
        [
            q_part.reshape(seq_count, -1),
            k_part.reshape(seq_count, -1),
            v_part.reshape(seq_count, -1),
            jnp.broadcast_to(codes, (seq_count, 128)),
        ],
        axis=1,
    )
    recv = lax.all_to_all(send, "seq", 0, 0, tiled=True)
    q_len = tok_rows * heads_dev * HD
    kv_len = tok_rows * HD
    query_block = recv[:, :q_len].reshape(seq_count * tok_rows, heads_dev, HD)
    slab_k = recv[:, q_len : q_len + kv_len].reshape(seq_count * tok_rows, HD)
    slab_v = recv[:, q_len + kv_len : q_len + 2 * kv_len].reshape(seq_count * tok_rows, HD)
    got_codes = recv[:, q_len + 2 * kv_len : q_len + 2 * kv_len + tok_rows * 2]
    got_codes = got_codes.reshape(seq_count * tok_rows, 2).astype(jnp.float32)
    own_pos = got_codes[:, 0] * code_base + got_codes[:, 1]

    code_row = jnp.pad(got_codes.T.reshape(1, -1).astype(jnp.bfloat16), ((0, 0), (0, 2 * HD - 2 * seq_count * tok_rows)))
    slab_block = jnp.concatenate([jnp.concatenate([slab_k, slab_v], axis=1), code_row], axis=0)
    slab_all = gather_cells(slab_block, cell_axes, cell_count)
    slab_rows = seq_count * tok_rows
    keys_new = slab_all[:, :slab_rows, :HD].reshape(-1, HD)
    values_new = slab_all[:, :slab_rows, HD:].reshape(-1, HD)
    key_codes = slab_all[:, slab_rows, : 2 * slab_rows].reshape(cell_count, 2, slab_rows).astype(jnp.float32)
    key_pos_new = (key_codes[:, 0] * code_base + key_codes[:, 1]).reshape(-1)

    cache_block = jnp.concatenate(
        [
            lax.dynamic_slice_in_dim(cache_keys, kv_first * HD, HD, 1),
            lax.dynamic_slice_in_dim(cache_values, kv_first * HD, HD, 1),
        ],
        axis=1,
    )
    cache_all = gather_cells(cache_block, cell_axes, cell_count).reshape(-1, 2 * HD)
    keys = jnp.concatenate([cache_all[:, :HD], keys_new], axis=0)
    values = jnp.concatenate([cache_all[:, HD:], values_new], axis=0)

    cache_rows = cache_all.shape[0]
    row_ids = jnp.arange(cache_rows, dtype=jnp.int32)
    cache_ok = jnp.broadcast_to((row_ids < first_pos)[None, :], (own_pos.shape[0], cache_rows))
    slab_ok = key_pos_new[None, :] <= own_pos[:, None]
    allowed = jnp.concatenate([cache_ok, slab_ok], axis=1)[:, None, :]

    score_scale = 1.0 / math.sqrt(HD)
    scores = jnp.einsum("thd,nd->thn", query_block, keys, preferred_element_type=jnp.float32) * score_scale
    row_max = jnp.max(jnp.where(allowed, scores, -jnp.inf), axis=-1, keepdims=True)
    exponent = jnp.where(allowed, jnp.exp(scores - row_max), 0.0)
    denominator = jnp.sum(exponent, axis=-1, keepdims=True)
    summed = jnp.einsum(
        "thn,nd->thd", exponent.astype(jnp.bfloat16), values, preferred_element_type=jnp.float32
    )
    context = (summed / denominator).astype(jnp.bfloat16).reshape(slab_rows, heads_dev * HD)
    return lax.all_to_all(context, "seq", split_axis=0, concat_axis=1, tiled=True)


def solution(mesh):
    in_specs = (
        P(("seq", "row", "col"), None),
        P(("seq", "row", "col"), None),
        P(("seq", "row", "col"), None),
        P(("seq", "row", "col")),
        P(("row", "col"), None),
        P(("row", "col"), None),
        P(),
    )
    out_specs = P(("seq", "row", "col"), None)
    return jax.shard_map(
        on_device, mesh=mesh, in_specs=in_specs, out_specs=out_specs, check_vma=False
    )
```

```python
import math

import numpy as np
import jax
import jax.numpy as jnp
from jax import lax
from jax.sharding import PartitionSpec as P

HQ = 64
KVH = 8
HD = 128

far_position = 1073741824
code_base = 256


def gather_cells(block, cell_axes, cell_count):
    spread = jnp.broadcast_to(block[None], (cell_count,) + block.shape)
    return lax.all_to_all(spread, cell_axes, 0, 0, tiled=True)


def pick_heads(rows, kv_of_peer, tok_rows):
    split = rows.reshape(tok_rows, KVH, 1, HD)
    repeat = kv_of_peer.shape[0] // KVH
    if repeat * KVH == kv_of_peer.shape[0] and np.array_equal(kv_of_peer, np.arange(kv_of_peer.shape[0]) // repeat):
        spread = jnp.broadcast_to(split, (tok_rows, KVH, repeat, HD)).reshape(tok_rows, -1, HD)
    else:
        spread = jnp.take(split[:, :, 0], kv_of_peer, axis=1)
    return spread.transpose(1, 0, 2)


def on_device(queries, new_keys, new_values, positions, cache_keys, cache_values, slab_start):
    seq_count = lax.axis_size("seq")
    cell_axes = ("row", "col")
    cell_count = lax.axis_size("row") * lax.axis_size("col")
    heads_dev = HQ // seq_count
    group_size = HQ // KVH
    tok_rows = queries.shape[0]
    first_pos = slab_start[0]

    kv_of_peer = np.arange(seq_count) * heads_dev // group_size
    kv_first = lax.axis_index("seq") * heads_dev // group_size

    q_part = queries.reshape(tok_rows, seq_count, heads_dev * HD).transpose(1, 0, 2)
    k_part = pick_heads(new_keys, kv_of_peer, tok_rows)
    v_part = pick_heads(new_values, kv_of_peer, tok_rows)
    codes = jnp.stack([positions // code_base, positions % code_base], axis=1).astype(jnp.bfloat16)
    codes = jnp.pad(codes.reshape(1, tok_rows * 2), ((0, 0), (0, 128 - tok_rows * 2)))
    send = jnp.concatenate(
        [
            q_part.reshape(seq_count, -1),
            k_part.reshape(seq_count, -1),
            v_part.reshape(seq_count, -1),
            jnp.broadcast_to(codes, (seq_count, 128)),
        ],
        axis=1,
    )
    recv = lax.all_to_all(send, "seq", 0, 0, tiled=True)
    q_len = tok_rows * heads_dev * HD
    kv_len = tok_rows * HD
    query_block = recv[:, :q_len].reshape(seq_count * tok_rows, heads_dev, HD)
    slab_k = recv[:, q_len : q_len + kv_len].reshape(seq_count * tok_rows, HD)
    slab_v = recv[:, q_len + kv_len : q_len + 2 * kv_len].reshape(seq_count * tok_rows, HD)
    got_codes = recv[:, q_len + 2 * kv_len : q_len + 2 * kv_len + tok_rows * 2]
    got_codes = got_codes.reshape(seq_count * tok_rows, 2).astype(jnp.float32)
    own_pos = got_codes[:, 0] * code_base + got_codes[:, 1]

    code_row = jnp.pad(got_codes.T.reshape(1, -1).astype(jnp.bfloat16), ((0, 0), (0, 2 * HD - 2 * seq_count * tok_rows)))
    cache_block = jnp.concatenate(
        [
            lax.dynamic_slice_in_dim(cache_keys, kv_first * HD, HD, 1),
            lax.dynamic_slice_in_dim(cache_values, kv_first * HD, HD, 1),
        ],
        axis=1,
    )
    cache_len = cache_block.shape[0]
    slab_rows = seq_count * tok_rows
    block = jnp.concatenate([cache_block, jnp.concatenate([slab_k, slab_v], axis=1), code_row], axis=0)
    every = gather_cells(block, cell_axes, cell_count)
    cache_all = every[:, :cache_len].reshape(-1, 2 * HD)
    keys_new = every[:, cache_len : cache_len + slab_rows, :HD].reshape(-1, HD)
    values_new = every[:, cache_len : cache_len + slab_rows, HD:].reshape(-1, HD)
    key_codes = every[:, cache_len + slab_rows, : 2 * slab_rows].reshape(cell_count, 2, slab_rows).astype(jnp.float32)
    key_pos_new = (key_codes[:, 0] * code_base + key_codes[:, 1]).reshape(-1)
    keys = jnp.concatenate([cache_all[:, :HD], keys_new], axis=0)
    values = jnp.concatenate([cache_all[:, HD:], values_new], axis=0)

    cache_rows = cache_all.shape[0]
    row_ids = jnp.arange(cache_rows, dtype=jnp.int32)
    cache_ok = jnp.broadcast_to((row_ids < first_pos)[None, :], (own_pos.shape[0], cache_rows))
    slab_ok = key_pos_new[None, :] <= own_pos[:, None]
    allowed = jnp.concatenate([cache_ok, slab_ok], axis=1)[:, None, :]

    score_scale = 1.0 / math.sqrt(HD)
    scores = jnp.einsum("thd,nd->thn", query_block, keys, preferred_element_type=jnp.float32) * score_scale
    row_max = jnp.max(jnp.where(allowed, scores, -jnp.inf), axis=-1, keepdims=True)
    exponent = jnp.where(allowed, jnp.exp(scores - row_max), 0.0)
    denominator = jnp.sum(exponent, axis=-1, keepdims=True)
    summed = jnp.einsum(
        "thn,nd->thd", exponent.astype(jnp.bfloat16), values, preferred_element_type=jnp.float32
    )
    context = (summed / denominator).astype(jnp.bfloat16).reshape(slab_rows, heads_dev * HD)
    return lax.all_to_all(context, "seq", split_axis=0, concat_axis=1, tiled=True)


def solution(mesh):
    in_specs = (
        P(("seq", "row", "col"), None),
        P(("seq", "row", "col"), None),
        P(("seq", "row", "col"), None),
        P(("seq", "row", "col")),
        P(("row", "col"), None),
        P(("row", "col"), None),
        P(),
    )
    out_specs = P(("seq", "row", "col"), None)
    return jax.shard_map(
        on_device, mesh=mesh, in_specs=in_specs, out_specs=out_specs, check_vma=False
    )
```

```python
import math

import numpy as np
import jax
import jax.numpy as jnp
from jax import lax
from jax.sharding import PartitionSpec as P

HQ = 64
KVH = 8
HD = 128

far_position = 1073741824
code_base = 256


def gather_cells(block, cell_axes, cell_count):
    spread = jnp.broadcast_to(block[None], (cell_count,) + block.shape)
    return lax.all_to_all(spread, cell_axes, 0, 0, tiled=True)


def pick_heads(rows, kv_of_peer, tok_rows, width=HD):
    split = rows.reshape(tok_rows, KVH, 1, width)
    repeat = kv_of_peer.shape[0] // KVH
    if repeat * KVH == kv_of_peer.shape[0] and np.array_equal(kv_of_peer, np.arange(kv_of_peer.shape[0]) // repeat):
        spread = jnp.broadcast_to(split, (tok_rows, KVH, repeat, width)).reshape(tok_rows, -1, width)
    else:
        spread = jnp.take(split[:, :, 0], kv_of_peer, axis=1)
    return spread.transpose(1, 0, 2)


def on_device(queries, new_keys, new_values, positions, cache_keys, cache_values, slab_start):
    seq_count = lax.axis_size("seq")
    cell_axes = ("row", "col")
    cell_count = lax.axis_size("row") * lax.axis_size("col")
    cell_index = lax.axis_index("row") * lax.axis_size("col") + lax.axis_index("col")
    heads_dev = HQ // seq_count
    group_size = HQ // KVH
    tok_rows = queries.shape[0]
    first_pos = slab_start[0]
    kv_of_peer = np.arange(seq_count) * heads_dev // group_size
    kv_first = lax.axis_index("seq") * heads_dev // group_size
    width = 2 * HD

    cache_block = jnp.concatenate(
        [
            lax.dynamic_slice_in_dim(cache_keys, kv_first * HD, HD, 1),
            lax.dynamic_slice_in_dim(cache_values, kv_first * HD, HD, 1),
        ],
        axis=1,
    )
    cache_len = cache_block.shape[0]
    local_kv = jnp.concatenate([new_keys, new_values], axis=1).reshape(-1, width)
    kv_len = local_kv.shape[0]
    codes = jnp.stack([positions // code_base, positions % code_base], axis=1).astype(jnp.bfloat16)
    code_row = jnp.pad(codes.reshape(1, tok_rows * 2), ((0, 0), (0, width - tok_rows * 2)))
    block = jnp.concatenate([cache_block, local_kv, code_row], axis=0)
    every = gather_cells(block, cell_axes, cell_count)
    cache_all = every[:, :cache_len].reshape(-1, width)
    slice_rows = cell_count * tok_rows
    slice_kv = every[:, cache_len : cache_len + kv_len].reshape(slice_rows, 2, KVH, HD)
    slice_codes = every[:, cache_len + kv_len, : tok_rows * 2].reshape(1, slice_rows * 2)

    q_part = queries.reshape(tok_rows, seq_count, heads_dev * HD).transpose(1, 0, 2).reshape(seq_count, -1)
    kv_part = pick_heads(slice_kv.transpose(0, 2, 1, 3).reshape(slice_rows, KVH * width), kv_of_peer, slice_rows, width)
    send = jnp.concatenate(
        [q_part, kv_part.reshape(seq_count, -1), jnp.broadcast_to(slice_codes, (seq_count, slice_rows * 2))],
        axis=1,
    )
    recv = lax.all_to_all(send, "seq", 0, 0, tiled=True)
    q_len = q_part.shape[1]
    kvp_len = slice_rows * width
    query_block = recv[:, :q_len].reshape(seq_count * tok_rows, heads_dev, HD)
    slab_kv = recv[:, q_len : q_len + kvp_len].reshape(seq_count * slice_rows, width)
    key_codes = recv[:, q_len + kvp_len :].reshape(seq_count, cell_count, tok_rows, 2).astype(jnp.float32)
    key_pos_new = (key_codes[..., 0] * code_base + key_codes[..., 1]).reshape(-1)
    own_codes = lax.dynamic_index_in_dim(key_codes, cell_index, 1, keepdims=False).reshape(-1, 2)
    own_pos = own_codes[:, 0] * code_base + own_codes[:, 1]

    keys = jnp.concatenate([cache_all[:, :HD], slab_kv[:, :HD]], axis=0)
    values = jnp.concatenate([cache_all[:, HD:], slab_kv[:, HD:]], axis=0)

    cache_rows = cache_all.shape[0]
    row_ids = jnp.arange(cache_rows, dtype=jnp.int32)
    cache_ok = jnp.broadcast_to((row_ids < first_pos)[None, :], (own_pos.shape[0], cache_rows))
    slab_ok = key_pos_new[None, :] <= own_pos[:, None]
    allowed = jnp.concatenate([cache_ok, slab_ok], axis=1)[:, None, :]

    score_scale = 1.0 / math.sqrt(HD)
    scores = jnp.einsum("thd,nd->thn", query_block, keys, preferred_element_type=jnp.float32) * score_scale
    row_max = jnp.max(jnp.where(allowed, scores, -jnp.inf), axis=-1, keepdims=True)
    exponent = jnp.where(allowed, jnp.exp(scores - row_max), 0.0)
    denominator = jnp.sum(exponent, axis=-1, keepdims=True)
    summed = jnp.einsum(
        "thn,nd->thd", exponent.astype(jnp.bfloat16), values, preferred_element_type=jnp.float32
    )
    context = (summed / denominator).astype(jnp.bfloat16).reshape(seq_count * tok_rows, heads_dev * HD)
    return lax.all_to_all(context, "seq", split_axis=0, concat_axis=1, tiled=True)


def solution(mesh):
    in_specs = (
        P(("seq", "row", "col"), None),
        P(("seq", "row", "col"), None),
        P(("seq", "row", "col"), None),
        P(("seq", "row", "col")),
        P(("row", "col"), None),
        P(("row", "col"), None),
        P(),
    )
    out_specs = P(("seq", "row", "col"), None)
    return jax.shard_map(
        on_device, mesh=mesh, in_specs=in_specs, out_specs=out_specs, check_vma=False
    )
```

```python
import math

import numpy as np
import jax
import jax.numpy as jnp
from jax import lax
from jax.sharding import PartitionSpec as P

HQ = 64
KVH = 8
HD = 128

far_position = 1073741824
code_base = 256


def gather_cells(block, cell_axes, cell_count):
    spread = jnp.broadcast_to(block[None], (cell_count,) + block.shape)
    return lax.all_to_all(spread, cell_axes, 0, 0, tiled=True)


def pick_heads(rows, kv_of_peer, tok_rows):
    split = rows.reshape(tok_rows, KVH, 1, HD)
    repeat = kv_of_peer.shape[0] // KVH
    if repeat * KVH == kv_of_peer.shape[0] and np.array_equal(kv_of_peer, np.arange(kv_of_peer.shape[0]) // repeat):
        spread = jnp.broadcast_to(split, (tok_rows, KVH, repeat, HD)).reshape(tok_rows, -1, HD)
    else:
        spread = jnp.take(split[:, :, 0], kv_of_peer, axis=1)
    return spread.transpose(1, 0, 2)


def partner_swap(x, pairs):
    return lax.ppermute(x, "row", pairs)


def partial_attention(query_block, query_pos, keys, values, key_pos_cache, key_pos_slab, cache_rows, first_pos):
    cache_ok = jnp.broadcast_to((key_pos_cache < first_pos)[None, :], (query_pos.shape[0], cache_rows))
    slab_ok = key_pos_slab[None, :] <= query_pos[:, None]
    allowed = jnp.concatenate([cache_ok, slab_ok], axis=1)[:, None, :]
    score_scale = 1.0 / math.sqrt(HD)
    scores = jnp.einsum("thd,nd->thn", query_block, keys, preferred_element_type=jnp.float32) * score_scale
    row_max = jnp.max(jnp.where(allowed, scores, -jnp.inf), axis=-1)
    exponent = jnp.where(allowed, jnp.exp(scores - row_max[..., None]), 0.0)
    row_sum = jnp.sum(exponent, axis=-1)
    summed = jnp.einsum(
        "thn,nd->thd", exponent.astype(jnp.bfloat16), values, preferred_element_type=jnp.float32
    )
    return row_max, row_sum, summed


def on_device(queries, new_keys, new_values, positions, cache_keys, cache_values, slab_start):
    seq_count = lax.axis_size("seq")
    cell_axes = ("row", "col")
    row_count = lax.axis_size("row")
    col_count = lax.axis_size("col")
    cell_count = row_count * col_count
    heads_dev = HQ // seq_count
    group_size = HQ // KVH
    tok_rows = queries.shape[0]
    first_pos = slab_start[0]
    kv_of_peer = np.arange(seq_count) * heads_dev // group_size
    kv_first = lax.axis_index("seq") * heads_dev // group_size
    core = lax.axis_index("row") % 2
    pairs = [(r, r ^ 1) for r in range(row_count)]
    width = 2 * HD

    q_part = queries.reshape(tok_rows, seq_count, heads_dev * HD).transpose(1, 0, 2)
    k_part = pick_heads(new_keys, kv_of_peer, tok_rows)
    v_part = pick_heads(new_values, kv_of_peer, tok_rows)
    codes = jnp.stack([positions // code_base, positions % code_base], axis=1).astype(jnp.bfloat16)
    codes = jnp.pad(codes.reshape(1, tok_rows * 2), ((0, 0), (0, 128 - tok_rows * 2)))
    send = jnp.concatenate(
        [
            q_part.reshape(seq_count, -1),
            k_part.reshape(seq_count, -1),
            v_part.reshape(seq_count, -1),
            jnp.broadcast_to(codes, (seq_count, 128)),
        ],
        axis=1,
    )
    recv = lax.all_to_all(send, "seq", 0, 0, tiled=True)
    q_len = tok_rows * heads_dev * HD
    kv_len = tok_rows * HD
    slab_rows = seq_count * tok_rows
    query_block = recv[:, :q_len].reshape(slab_rows, heads_dev, HD)
    slab_k = recv[:, q_len : q_len + kv_len].reshape(slab_rows, HD)
    slab_v = recv[:, q_len + kv_len : q_len + 2 * kv_len].reshape(slab_rows, HD)
    got_codes = recv[:, q_len + 2 * kv_len : q_len + 2 * kv_len + tok_rows * 2]
    got_codes = got_codes.reshape(slab_rows, 2)
    own_pos = got_codes[:, 0].astype(jnp.float32) * code_base + got_codes[:, 1].astype(jnp.float32)

    partner_q = partner_swap(jnp.concatenate([query_block.reshape(slab_rows, -1), got_codes], axis=1), pairs)
    partner_block = partner_q[:, : heads_dev * HD].reshape(slab_rows, heads_dev, HD)
    partner_codes = partner_q[:, heads_dev * HD :].astype(jnp.float32)
    partner_pos = partner_codes[:, 0] * code_base + partner_codes[:, 1]

    cache_block = jnp.concatenate(
        [
            lax.dynamic_slice_in_dim(cache_keys, kv_first * HD, HD, 1),
            lax.dynamic_slice_in_dim(cache_values, kv_first * HD, HD, 1),
        ],
        axis=1,
    )
    cache_len = cache_block.shape[0]
    half_cache = cache_len // 2
    half_slab = slab_rows // 2
    slab_kv = jnp.concatenate([slab_k, slab_v], axis=1)
    code_rows = jnp.pad(got_codes.reshape(2, half_slab * 2), ((0, 0), (0, width - half_slab * 2)))
    halves = jnp.stack(
        [
            jnp.concatenate(
                [cache_block[b * half_cache : (b + 1) * half_cache], slab_kv[b * half_slab : (b + 1) * half_slab], code_rows[b : b + 1]],
                axis=0,
            )
            for b in range(2)
        ]
    )
    per_dest = jnp.broadcast_to(
        halves[None, :, None], (row_count // 2, 2, col_count) + halves.shape[1:]
    ).reshape((cell_count,) + halves.shape[1:])
    every = lax.all_to_all(per_dest, cell_axes, 0, 0, tiled=True)
    cache_got = every[:, :half_cache].reshape(-1, width)
    slab_got = every[:, half_cache : half_cache + half_slab].reshape(-1, width)
    key_codes = every[:, half_cache + half_slab, : 2 * half_slab].reshape(-1, 2).astype(jnp.float32)
    key_pos_slab = key_codes[:, 0] * code_base + key_codes[:, 1]
    key_pos_cache = (
        jnp.arange(cell_count, dtype=jnp.int32)[:, None] * cache_len
        + core * half_cache
        + jnp.arange(half_cache, dtype=jnp.int32)[None, :]
    ).reshape(-1)
    keys = jnp.concatenate([cache_got[:, :HD], slab_got[:, :HD]], axis=0)
    values = jnp.concatenate([cache_got[:, HD:], slab_got[:, HD:]], axis=0)

    both_q = jnp.concatenate([query_block, partner_block], axis=0)
    both_pos = jnp.concatenate([own_pos, partner_pos], axis=0)
    row_max, row_sum, summed = partial_attention(
        both_q, both_pos, keys, values, key_pos_cache, key_pos_slab, cache_got.shape[0], first_pos
    )
    theirs = jnp.concatenate(
        [summed[slab_rows:].reshape(slab_rows, -1), row_max[slab_rows:], row_sum[slab_rows:]], axis=1
    )
    got = partner_swap(theirs, pairs)
    other_summed = got[:, : heads_dev * HD].reshape(slab_rows, heads_dev, HD)
    other_max = got[:, heads_dev * HD : heads_dev * HD + heads_dev]
    other_sum = got[:, heads_dev * HD + heads_dev :]
    mine_max = row_max[:slab_rows]
    top = jnp.maximum(mine_max, other_max)
    scale_mine = jnp.exp(mine_max - top)
    scale_other = jnp.exp(other_max - top)
    numerator = summed[:slab_rows] * scale_mine[..., None] + other_summed * scale_other[..., None]
    denominator = row_sum[:slab_rows] * scale_mine + other_sum * scale_other
    context = (numerator / denominator[..., None]).astype(jnp.bfloat16).reshape(slab_rows, heads_dev * HD)
    return lax.all_to_all(context, "seq", split_axis=0, concat_axis=1, tiled=True)


def solution(mesh):
    in_specs = (
        P(("seq", "row", "col"), None),
        P(("seq", "row", "col"), None),
        P(("seq", "row", "col"), None),
        P(("seq", "row", "col")),
        P(("row", "col"), None),
        P(("row", "col"), None),
        P(),
    )
    out_specs = P(("seq", "row", "col"), None)
    return jax.shard_map(
        on_device, mesh=mesh, in_specs=in_specs, out_specs=out_specs, check_vma=False
    )
```

```python
import math

import numpy as np
import jax
import jax.numpy as jnp
from jax import lax
from jax.sharding import PartitionSpec as P

HQ = 64
KVH = 8
HD = 128

far_position = 1073741824
code_base = 256


def gather_cells(block, cell_axes, cell_count):
    spread = jnp.broadcast_to(block[None], (cell_count,) + block.shape)
    return lax.all_to_all(spread, cell_axes, 0, 0, tiled=True)


def pick_heads(rows, kv_of_peer, tok_rows):
    split = rows.reshape(tok_rows, KVH, 1, HD)
    repeat = kv_of_peer.shape[0] // KVH
    if repeat * KVH == kv_of_peer.shape[0] and np.array_equal(kv_of_peer, np.arange(kv_of_peer.shape[0]) // repeat):
        spread = jnp.broadcast_to(split, (tok_rows, KVH, repeat, HD)).reshape(tok_rows, -1, HD)
    else:
        spread = jnp.take(split[:, :, 0], kv_of_peer, axis=1)
    return spread.transpose(1, 0, 2)


def partner_swap(x, pairs):
    return lax.ppermute(x, "row", pairs)


def partial_attention(query_block, query_pos, keys, values, key_pos_cache, key_pos_slab, cache_rows, first_pos):
    cache_ok = jnp.broadcast_to((key_pos_cache < first_pos)[None, :], (query_pos.shape[0], cache_rows))
    slab_ok = key_pos_slab[None, :] <= query_pos[:, None]
    allowed = jnp.concatenate([cache_ok, slab_ok], axis=1)[:, None, :]
    score_scale = 1.0 / math.sqrt(HD)
    scores = jnp.einsum("thd,nd->thn", query_block, keys, preferred_element_type=jnp.float32) * score_scale
    row_max = jnp.max(jnp.where(allowed, scores, -jnp.inf), axis=-1)
    exponent = jnp.where(allowed, jnp.exp(scores - row_max[..., None]), 0.0)
    row_sum = jnp.sum(exponent, axis=-1)
    summed = jnp.einsum(
        "thn,nd->thd", exponent.astype(jnp.bfloat16), values, preferred_element_type=jnp.float32
    )
    return row_max, row_sum, summed


def swap(x, axes, pairs):
    return lax.ppermute(x, axes, pairs)


def decode(codes):
    codes = codes.astype(jnp.float32)
    return codes[..., 0] * code_base + codes[..., 1]


def on_device(queries, new_keys, new_values, positions, cache_keys, cache_values, slab_start):
    seq_count = lax.axis_size("seq")
    cell_axes = ("row", "col")
    row_count = lax.axis_size("row")
    col_count = lax.axis_size("col")
    cell_count = row_count * col_count
    heads_dev = HQ // seq_count
    group_size = HQ // KVH
    tok_rows = queries.shape[0]
    first_pos = slab_start[0]
    seq_index = lax.axis_index("seq")
    kv_first = seq_index * heads_dev // group_size
    parity = seq_index % 2
    core = lax.axis_index("row") % 2
    quarter = parity * 2 + core
    core_pairs = [(r, r ^ 1) for r in range(row_count)]
    seq_pairs = [(q, q ^ 1) for q in range(seq_count)]
    diag_pairs = [(q * row_count + r, (q ^ 1) * row_count + (r ^ 1)) for q in range(seq_count) for r in range(row_count)]
    width = 2 * HD
    pair_heads = 2 * heads_dev
    half_tok = tok_rows // 2

    q_pairs = queries.reshape(tok_rows, seq_count // 2, 1, pair_heads * HD)
    q_part = jnp.broadcast_to(q_pairs, (tok_rows, seq_count // 2, 2, pair_heads * HD)).reshape(tok_rows, seq_count, -1)
    kv_local = jnp.concatenate(
        [new_keys.reshape(tok_rows, KVH, 1, HD), new_values.reshape(tok_rows, KVH, 1, HD)], axis=2
    ).reshape(2, half_tok, KVH, 1, width)
    repeat = seq_count // (2 * KVH)
    kv_part = jnp.broadcast_to(
        kv_local.transpose(2, 3, 0, 1, 4)[:, :, None], (KVH, 1, repeat, 2, half_tok, width)
    ).reshape(seq_count, half_tok * width)
    codes = jnp.stack([positions // code_base, positions % code_base], axis=1).astype(jnp.bfloat16)
    codes = jnp.pad(codes.reshape(1, tok_rows * 2), ((0, 0), (0, 128 - tok_rows * 2)))
    send = jnp.concatenate(
        [q_part.transpose(1, 0, 2).reshape(seq_count, -1), kv_part, jnp.broadcast_to(codes, (seq_count, 128))],
        axis=1,
    )
    recv = lax.all_to_all(send, "seq", 0, 0, tiled=True)
    q_len = tok_rows * pair_heads * HD
    kvp_len = half_tok * width
    slab_rows = seq_count * tok_rows
    query_block = recv[:, :q_len].reshape(slab_rows, pair_heads, HD)
    slab_kv = recv[:, q_len : q_len + kvp_len].reshape(seq_count * half_tok, width)
    got_codes = recv[:, q_len + kvp_len : q_len + kvp_len + tok_rows * 2].reshape(seq_count, tok_rows, 2)
    own_pos = decode(got_codes.reshape(slab_rows, 2))
    slab_codes = lax.dynamic_slice_in_dim(got_codes, parity * half_tok, half_tok, 1).reshape(seq_count * half_tok, 2)

    partner_q = swap(
        jnp.concatenate([query_block.reshape(slab_rows, -1), got_codes.reshape(slab_rows, 2)], axis=1), "row", core_pairs
    )
    partner_block = partner_q[:, : pair_heads * HD].reshape(slab_rows, pair_heads, HD)
    partner_pos = decode(partner_q[:, pair_heads * HD :])

    cache_block = jnp.concatenate(
        [
            lax.dynamic_slice_in_dim(cache_keys, kv_first * HD, HD, 1),
            lax.dynamic_slice_in_dim(cache_values, kv_first * HD, HD, 1),
        ],
        axis=1,
    )
    cache_len = cache_block.shape[0]
    part_cache = cache_len // 4
    half_slab = slab_kv.shape[0] // 2
    code_rows = jnp.pad(slab_codes.reshape(2, half_slab * 2), ((0, 0), (0, width - half_slab * 2)))
    cache_pair = lax.dynamic_slice_in_dim(cache_block, parity * 2 * part_cache, 2 * part_cache, 0)
    halves = jnp.stack(
        [
            jnp.concatenate(
                [
                    cache_pair[b * part_cache : (b + 1) * part_cache],
                    slab_kv[b * half_slab : (b + 1) * half_slab],
                    code_rows[b : b + 1],
                ],
                axis=0,
            )
            for b in range(2)
        ]
    )
    per_dest = jnp.broadcast_to(
        halves[None, :, None], (row_count // 2, 2, col_count) + halves.shape[1:]
    ).reshape((cell_count,) + halves.shape[1:])
    every = lax.all_to_all(per_dest, cell_axes, 0, 0, tiled=True)
    cache_got = every[:, :part_cache].reshape(-1, width)
    slab_got = every[:, part_cache : part_cache + half_slab].reshape(-1, width)
    key_pos_slab = decode(every[:, part_cache + half_slab, : 2 * half_slab].reshape(-1, 2))
    key_pos_cache = (
        jnp.arange(cell_count, dtype=jnp.int32)[:, None] * cache_len
        + quarter * part_cache
        + jnp.arange(part_cache, dtype=jnp.int32)[None, :]
    ).reshape(-1)
    keys = jnp.concatenate([cache_got[:, :HD], slab_got[:, :HD]], axis=0)
    values = jnp.concatenate([cache_got[:, HD:], slab_got[:, HD:]], axis=0)

    both_q = jnp.concatenate([query_block, partner_block], axis=0)
    both_pos = jnp.concatenate([own_pos, partner_pos], axis=0)
    row_max, row_sum, summed = partial_attention(
        both_q, both_pos, keys, values, key_pos_cache, key_pos_slab, cache_got.shape[0], first_pos
    )

    def block(rows, pair):
        take = slice(rows * slab_rows, (rows + 1) * slab_rows)
        heads = pl_heads(pair, heads_dev)
        return jnp.concatenate(
            [
                lax.dynamic_slice_in_dim(summed[take], heads, heads_dev, 1).reshape(slab_rows, -1),
                lax.dynamic_slice_in_dim(row_max[take], heads, heads_dev, 1),
                lax.dynamic_slice_in_dim(row_sum[take], heads, heads_dev, 1),
            ],
            axis=1,
        )

    pieces = [
        block(0, parity),
        swap(block(1, parity), "row", core_pairs),
        swap(block(0, 1 - parity), "seq", seq_pairs),
        swap(block(1, 1 - parity), ("seq", "row"), diag_pairs),
    ]
    split_at = heads_dev * HD
    maxes = [p[:, split_at : split_at + heads_dev] for p in pieces]
    top = maxes[0]
    for m in maxes[1:]:
        top = jnp.maximum(top, m)
    numerator = 0.0
    denominator = 0.0
    for p, m in zip(pieces, maxes):
        factor = jnp.exp(m - top)
        numerator = numerator + p[:, :split_at].reshape(slab_rows, heads_dev, HD) * factor[..., None]
        denominator = denominator + p[:, split_at + heads_dev :] * factor
    context = (numerator / denominator[..., None]).astype(jnp.bfloat16).reshape(slab_rows, heads_dev * HD)
    return lax.all_to_all(context, "seq", split_axis=0, concat_axis=1, tiled=True)


def pl_heads(pair, heads_dev):
    return pair * heads_dev


def solution(mesh):
    in_specs = (
        P(("seq", "row", "col"), None),
        P(("seq", "row", "col"), None),
        P(("seq", "row", "col"), None),
        P(("seq", "row", "col")),
        P(("row", "col"), None),
        P(("row", "col"), None),
        P(),
    )
    out_specs = P(("seq", "row", "col"), None)
    return jax.shard_map(
        on_device, mesh=mesh, in_specs=in_specs, out_specs=out_specs, check_vma=False
    )
```

```python
import math

import numpy as np
import jax
import jax.numpy as jnp
from jax import lax
from jax.sharding import PartitionSpec as P

HQ = 64
KVH = 8
HD = 128

far_position = 1073741824
code_base = 256


def gather_cells(block, cell_axes, cell_count):
    spread = jnp.broadcast_to(block[None], (cell_count,) + block.shape)
    return lax.all_to_all(spread, cell_axes, 0, 0, tiled=True)


def pick_heads(rows, kv_of_peer, tok_rows):
    split = rows.reshape(tok_rows, KVH, 1, HD)
    repeat = kv_of_peer.shape[0] // KVH
    if repeat * KVH == kv_of_peer.shape[0] and np.array_equal(kv_of_peer, np.arange(kv_of_peer.shape[0]) // repeat):
        spread = jnp.broadcast_to(split, (tok_rows, KVH, repeat, HD)).reshape(tok_rows, -1, HD)
    else:
        spread = jnp.take(split[:, :, 0], kv_of_peer, axis=1)
    return spread.transpose(1, 0, 2)


def partner_swap(x, pairs):
    return lax.ppermute(x, "row", pairs)


def partial_attention(query_block, query_pos, keys, values, key_pos_cache, key_pos_slab, cache_rows, first_pos):
    cache_ok = jnp.broadcast_to((key_pos_cache < first_pos)[None, :], (query_pos.shape[0], cache_rows))
    slab_ok = key_pos_slab[None, :] <= query_pos[:, None]
    allowed = jnp.concatenate([cache_ok, slab_ok], axis=1)[:, None, :]
    score_scale = 1.0 / math.sqrt(HD)
    scores = jnp.einsum("thd,nd->thn", query_block, keys, preferred_element_type=jnp.float32) * score_scale
    row_max = jnp.max(jnp.where(allowed, scores, -jnp.inf), axis=-1)
    exponent = jnp.where(allowed, jnp.exp(scores - row_max[..., None]), 0.0)
    row_sum = jnp.sum(exponent, axis=-1)
    summed = jnp.einsum(
        "thn,nd->thd", exponent.astype(jnp.bfloat16), values, preferred_element_type=jnp.float32
    )
    return row_max, row_sum, summed


def swap(x, axes, pairs):
    return lax.ppermute(x, axes, pairs)


def decode(codes):
    codes = codes.astype(jnp.float32)
    return codes[..., 0] * code_base + codes[..., 1]


def on_device(queries, new_keys, new_values, positions, cache_keys, cache_values, slab_start):
    seq_count = lax.axis_size("seq")
    cell_axes = ("row", "col")
    row_count = lax.axis_size("row")
    col_count = lax.axis_size("col")
    cell_count = row_count * col_count
    heads_dev = HQ // seq_count
    group_size = HQ // KVH
    tok_rows = queries.shape[0]
    first_pos = slab_start[0]
    seq_index = lax.axis_index("seq")
    kv_first = seq_index * heads_dev // group_size
    parity = seq_index % 2
    core = lax.axis_index("row") % 2
    quarter = parity * 2 + core
    core_pairs = [(r, r ^ 1) for r in range(row_count)]
    seq_pairs = [(q, q ^ 1) for q in range(seq_count)]
    diag_pairs = [(q * row_count + r, (q ^ 1) * row_count + (r ^ 1)) for q in range(seq_count) for r in range(row_count)]
    width = 2 * HD
    pair_heads = 2 * heads_dev
    half_tok = tok_rows // 2

    q_pairs = queries.reshape(tok_rows, seq_count // 2, 1, pair_heads * HD)
    q_part = jnp.broadcast_to(q_pairs, (tok_rows, seq_count // 2, 2, pair_heads * HD)).reshape(tok_rows, seq_count, -1)
    kv_local = jnp.concatenate(
        [new_keys.reshape(tok_rows, KVH, 1, HD), new_values.reshape(tok_rows, KVH, 1, HD)], axis=2
    ).reshape(2, half_tok, KVH, 1, width)
    repeat = seq_count // (2 * KVH)
    kv_part = jnp.broadcast_to(
        kv_local.transpose(2, 3, 0, 1, 4)[:, :, None], (KVH, 1, repeat, 2, half_tok, width)
    ).reshape(seq_count, half_tok * width)
    codes = jnp.stack([positions // code_base, positions % code_base], axis=1).astype(jnp.bfloat16)
    codes = jnp.pad(codes.reshape(1, tok_rows * 2), ((0, 0), (0, 128 - tok_rows * 2)))
    send = jnp.concatenate(
        [q_part.transpose(1, 0, 2).reshape(seq_count, -1), kv_part, jnp.broadcast_to(codes, (seq_count, 128))],
        axis=1,
    )
    recv = lax.all_to_all(send, "seq", 0, 0, tiled=True)
    q_len = tok_rows * pair_heads * HD
    kvp_len = half_tok * width
    slab_rows = seq_count * tok_rows
    query_block = recv[:, :q_len].reshape(slab_rows, pair_heads, HD)
    slab_kv = recv[:, q_len : q_len + kvp_len].reshape(seq_count * half_tok, width)
    got_codes = recv[:, q_len + kvp_len : q_len + kvp_len + tok_rows * 2].reshape(seq_count, tok_rows, 2)
    own_pos = decode(got_codes.reshape(slab_rows, 2))
    slab_codes = lax.dynamic_slice_in_dim(got_codes, parity * half_tok, half_tok, 1).reshape(seq_count * half_tok, 2)

    partner_q = swap(
        jnp.concatenate([query_block.reshape(slab_rows, -1), got_codes.reshape(slab_rows, 2)], axis=1), "row", core_pairs
    )
    partner_block = partner_q[:, : pair_heads * HD].reshape(slab_rows, pair_heads, HD)
    partner_pos = decode(partner_q[:, pair_heads * HD :])

    cache_block = jnp.concatenate(
        [
            lax.dynamic_slice_in_dim(cache_keys, kv_first * HD, HD, 1),
            lax.dynamic_slice_in_dim(cache_values, kv_first * HD, HD, 1),
        ],
        axis=1,
    )
    cache_len = cache_block.shape[0]
    part_cache = cache_len // 4
    half_slab = slab_kv.shape[0] // 2
    code_rows = jnp.pad(slab_codes.reshape(2, half_slab * 2), ((0, 0), (0, width - half_slab * 2)))
    cache_pair = lax.dynamic_slice_in_dim(cache_block, parity * 2 * part_cache, 2 * part_cache, 0)
    halves = jnp.stack(
        [
            jnp.concatenate(
                [
                    cache_pair[b * part_cache : (b + 1) * part_cache],
                    slab_kv[b * half_slab : (b + 1) * half_slab],
                    code_rows[b : b + 1],
                ],
                axis=0,
            )
            for b in range(2)
        ]
    )
    per_dest = jnp.broadcast_to(
        halves[None, :, None], (row_count // 2, 2, col_count) + halves.shape[1:]
    ).reshape((cell_count,) + halves.shape[1:])
    every = lax.all_to_all(per_dest, cell_axes, 0, 0, tiled=True)
    cache_got = every[:, :part_cache].reshape(-1, width)
    slab_got = every[:, part_cache : part_cache + half_slab].reshape(-1, width)
    key_pos_slab = decode(every[:, part_cache + half_slab, : 2 * half_slab].reshape(-1, 2))
    key_pos_cache = (
        jnp.arange(cell_count, dtype=jnp.int32)[:, None] * cache_len
        + quarter * part_cache
        + jnp.arange(part_cache, dtype=jnp.int32)[None, :]
    ).reshape(-1)
    keys = jnp.concatenate([cache_got[:, :HD], slab_got[:, :HD]], axis=0)
    values = jnp.concatenate([cache_got[:, HD:], slab_got[:, HD:]], axis=0)

    both_q = jnp.concatenate([query_block, partner_block], axis=0)
    both_pos = jnp.concatenate([own_pos, partner_pos], axis=0)
    row_max, row_sum, summed = partial_attention(
        both_q, both_pos, keys, values, key_pos_cache, key_pos_slab, cache_got.shape[0], first_pos
    )

    theirs = jnp.concatenate(
        [summed[slab_rows:].reshape(slab_rows, -1), row_max[slab_rows:], row_sum[slab_rows:]], axis=1
    )
    got = swap(theirs, "row", core_pairs)
    split_at = pair_heads * HD
    other_summed = got[:, :split_at].reshape(slab_rows, pair_heads, HD)
    other_max = got[:, split_at : split_at + pair_heads]
    other_sum = got[:, split_at + pair_heads :]
    mine_max = row_max[:slab_rows]
    top = jnp.maximum(mine_max, other_max)
    scale_mine = jnp.exp(mine_max - top)
    scale_other = jnp.exp(other_max - top)
    numerator = summed[:slab_rows] * scale_mine[..., None] + other_summed * scale_other[..., None]
    denominator = row_sum[:slab_rows] * scale_mine + other_sum * scale_other
    partial = jnp.concatenate([numerator.reshape(slab_rows, -1), top, denominator], axis=1)

    back = lax.all_to_all(partial.reshape(seq_count, tok_rows, -1), "seq", 0, 0, tiled=True)
    back = back.reshape(seq_count // 2, 2, tok_rows, -1)
    half_num = back[..., :split_at].reshape(seq_count // 2, 2, tok_rows, pair_heads, HD)
    half_max = back[..., split_at : split_at + pair_heads]
    half_sum = back[..., split_at + pair_heads :]
    best = jnp.maximum(half_max[:, 0], half_max[:, 1])
    f0 = jnp.exp(half_max[:, 0] - best)
    f1 = jnp.exp(half_max[:, 1] - best)
    num = half_num[:, 0] * f0[..., None] + half_num[:, 1] * f1[..., None]
    den = half_sum[:, 0] * f0 + half_sum[:, 1] * f1
    context = (num / den[..., None]).astype(jnp.bfloat16)
    return context.transpose(1, 0, 2, 3).reshape(tok_rows, -1)


def pl_heads(pair, heads_dev):
    return pair * heads_dev


def solution(mesh):
    in_specs = (
        P(("seq", "row", "col"), None),
        P(("seq", "row", "col"), None),
        P(("seq", "row", "col"), None),
        P(("seq", "row", "col")),
        P(("row", "col"), None),
        P(("row", "col"), None),
        P(),
    )
    out_specs = P(("seq", "row", "col"), None)
    return jax.shard_map(
        on_device, mesh=mesh, in_specs=in_specs, out_specs=out_specs, check_vma=False
    )
```

```python
import math

import numpy as np
import jax
import jax.numpy as jnp
from jax import lax
from jax.sharding import PartitionSpec as P
from jax.experimental import pallas as pl

HQ = 64
KVH = 8
HD = 128

far_position = 1073741824
code_base = 256


def gather_cells(block, cell_axes, cell_count):
    spread = jnp.broadcast_to(block[None], (cell_count,) + block.shape)
    return lax.all_to_all(spread, cell_axes, 0, 0, tiled=True)


def pick_heads(rows, kv_of_peer, tok_rows):
    split = rows.reshape(tok_rows, KVH, 1, HD)
    repeat = kv_of_peer.shape[0] // KVH
    if repeat * KVH == kv_of_peer.shape[0] and np.array_equal(kv_of_peer, np.arange(kv_of_peer.shape[0]) // repeat):
        spread = jnp.broadcast_to(split, (tok_rows, KVH, repeat, HD)).reshape(tok_rows, -1, HD)
    else:
        spread = jnp.take(split[:, :, 0], kv_of_peer, axis=1)
    return spread.transpose(1, 0, 2)


def partner_swap(x, pairs):
    return lax.ppermute(x, "row", pairs)


def partial_attention(query_block, query_pos, keys, values, key_pos_cache, key_pos_slab, cache_rows, first_pos):
    cache_ok = jnp.broadcast_to((key_pos_cache < first_pos)[None, :], (query_pos.shape[0], cache_rows))
    slab_ok = key_pos_slab[None, :] <= query_pos[:, None]
    allowed = jnp.concatenate([cache_ok, slab_ok], axis=1)[:, None, :]
    score_scale = 1.0 / math.sqrt(HD)
    scores = jnp.einsum("thd,nd->thn", query_block, keys, preferred_element_type=jnp.float32) * score_scale
    row_max = jnp.max(jnp.where(allowed, scores, -jnp.inf), axis=-1)
    exponent = jnp.where(allowed, jnp.exp(scores - row_max[..., None]), 0.0)
    row_sum = jnp.sum(exponent, axis=-1)
    summed = jnp.einsum(
        "thn,nd->thd", exponent.astype(jnp.bfloat16), values, preferred_element_type=jnp.float32
    )
    return row_max, row_sum, summed


def swap(x, axes, pairs):
    return lax.ppermute(x, axes, pairs)


def decode(codes):
    codes = codes.astype(jnp.float32)
    return codes[..., 0] * code_base + codes[..., 1]


def attention_kernel(q_ref, qc_ref, k_ref, v_ref, kc_ref, o_ref, m_ref, l_ref):
    scores = lax.dot_general(
        q_ref[...], k_ref[...], (((1,), (1,)), ((), ())), preferred_element_type=jnp.float32
    ) * (1.0 / math.sqrt(HD))
    allowed = kc_ref[...] <= qc_ref[...]
    row_max = jnp.max(jnp.where(allowed, scores, -jnp.inf), axis=1, keepdims=True)
    exponent = jnp.where(allowed, jnp.exp(scores - row_max), 0.0)
    l_ref[...] = jnp.sum(exponent, axis=1, keepdims=True)
    m_ref[...] = row_max
    o_ref[...] = jnp.dot(exponent.astype(jnp.bfloat16), v_ref[...], preferred_element_type=jnp.float32)


def fused_attention(q, q_code, keys, values, key_code, block=256):
    rows, count = q.shape[0], keys.shape[0]
    block = min(block, rows)
    row_spec = pl.BlockSpec((block, HD), lambda i: (i, 0))
    col_spec = pl.BlockSpec((block, 1), lambda i: (i, 0))
    whole = pl.BlockSpec((count, HD), lambda i: (0, 0))
    return pl.pallas_call(
        attention_kernel,
        grid=(rows // block,),
        in_specs=[row_spec, col_spec, whole, whole, pl.BlockSpec((1, count), lambda i: (0, 0))],
        out_specs=[row_spec, col_spec, col_spec],
        out_shape=[
            jax.ShapeDtypeStruct((rows, HD), jnp.float32),
            jax.ShapeDtypeStruct((rows, 1), jnp.float32),
            jax.ShapeDtypeStruct((rows, 1), jnp.float32),
        ],
        cost_estimate=pl.CostEstimate(
            flops=4 * rows * count * HD, transcendentals=rows * count, bytes_accessed=2 * (rows + 2 * count) * HD + 4 * rows * HD
        ),
    )(q, q_code, keys, values, key_code)


def on_device(queries, new_keys, new_values, positions, cache_keys, cache_values, slab_start):
    seq_count = lax.axis_size("seq")
    cell_axes = ("row", "col")
    row_count = lax.axis_size("row")
    col_count = lax.axis_size("col")
    cell_count = row_count * col_count
    heads_dev = HQ // seq_count
    group_size = HQ // KVH
    tok_rows = queries.shape[0]
    first_pos = slab_start[0]
    seq_index = lax.axis_index("seq")
    kv_first = seq_index * heads_dev // group_size
    parity = seq_index % 2
    core = lax.axis_index("row") % 2
    quarter = parity * 2 + core
    core_pairs = [(r, r ^ 1) for r in range(row_count)]
    seq_pairs = [(q, q ^ 1) for q in range(seq_count)]
    diag_pairs = [(q * row_count + r, (q ^ 1) * row_count + (r ^ 1)) for q in range(seq_count) for r in range(row_count)]
    width = 2 * HD
    pair_heads = 2 * heads_dev
    half_tok = tok_rows // 2

    q_pairs = queries.reshape(tok_rows, seq_count // 2, 1, pair_heads * HD)
    q_part = jnp.broadcast_to(q_pairs, (tok_rows, seq_count // 2, 2, pair_heads * HD)).reshape(tok_rows, seq_count, -1)
    kv_local = jnp.concatenate(
        [new_keys.reshape(tok_rows, KVH, 1, HD), new_values.reshape(tok_rows, KVH, 1, HD)], axis=2
    ).reshape(2, half_tok, KVH, 1, width)
    repeat = seq_count // (2 * KVH)
    kv_part = jnp.broadcast_to(
        kv_local.transpose(2, 3, 0, 1, 4)[:, :, None], (KVH, 1, repeat, 2, half_tok, width)
    ).reshape(seq_count, half_tok * width)
    codes = jnp.stack([positions // code_base, positions % code_base], axis=1).astype(jnp.bfloat16)
    codes = jnp.pad(codes.reshape(1, tok_rows * 2), ((0, 0), (0, 128 - tok_rows * 2)))
    send = jnp.concatenate(
        [q_part.transpose(1, 0, 2).reshape(seq_count, -1), kv_part, jnp.broadcast_to(codes, (seq_count, 128))],
        axis=1,
    )
    recv = lax.all_to_all(send, "seq", 0, 0, tiled=True)
    q_len = tok_rows * pair_heads * HD
    kvp_len = half_tok * width
    slab_rows = seq_count * tok_rows
    query_block = recv[:, :q_len].reshape(slab_rows, pair_heads, HD)
    slab_kv = recv[:, q_len : q_len + kvp_len].reshape(seq_count * half_tok, width)
    got_codes = recv[:, q_len + kvp_len : q_len + kvp_len + tok_rows * 2].reshape(seq_count, tok_rows, 2)
    own_pos = decode(got_codes.reshape(slab_rows, 2))
    slab_codes = lax.dynamic_slice_in_dim(got_codes, parity * half_tok, half_tok, 1).reshape(seq_count * half_tok, 2)

    partner_q = swap(
        jnp.concatenate([query_block.reshape(slab_rows, -1), got_codes.reshape(slab_rows, 2)], axis=1), "row", core_pairs
    )
    partner_block = partner_q[:, : pair_heads * HD].reshape(slab_rows, pair_heads, HD)
    partner_pos = decode(partner_q[:, pair_heads * HD :])

    cache_block = jnp.concatenate(
        [
            lax.dynamic_slice_in_dim(cache_keys, kv_first * HD, HD, 1),
            lax.dynamic_slice_in_dim(cache_values, kv_first * HD, HD, 1),
        ],
        axis=1,
    )
    cache_len = cache_block.shape[0]
    part_cache = cache_len // 4
    half_slab = slab_kv.shape[0] // 2
    code_rows = jnp.pad(slab_codes.reshape(2, half_slab * 2), ((0, 0), (0, width - half_slab * 2)))
    cache_pair = lax.dynamic_slice_in_dim(cache_block, parity * 2 * part_cache, 2 * part_cache, 0)
    halves = jnp.stack(
        [
            jnp.concatenate(
                [
                    cache_pair[b * part_cache : (b + 1) * part_cache],
                    slab_kv[b * half_slab : (b + 1) * half_slab],
                    code_rows[b : b + 1],
                ],
                axis=0,
            )
            for b in range(2)
        ]
    )
    per_dest = jnp.broadcast_to(
        halves[None, :, None], (row_count // 2, 2, col_count) + halves.shape[1:]
    ).reshape((cell_count,) + halves.shape[1:])
    every = lax.all_to_all(per_dest, cell_axes, 0, 0, tiled=True)
    cache_got = every[:, :part_cache].reshape(-1, width)
    slab_got = every[:, part_cache : part_cache + half_slab].reshape(-1, width)
    key_pos_slab = decode(every[:, part_cache + half_slab, : 2 * half_slab].reshape(-1, 2))
    key_pos_cache = (
        jnp.arange(cell_count, dtype=jnp.int32)[:, None] * cache_len
        + quarter * part_cache
        + jnp.arange(part_cache, dtype=jnp.int32)[None, :]
    ).reshape(-1)
    keys = jnp.concatenate([cache_got[:, :HD], slab_got[:, :HD]], axis=0)
    values = jnp.concatenate([cache_got[:, HD:], slab_got[:, HD:]], axis=0)

    both_q = jnp.concatenate([query_block, partner_block], axis=0)
    both_pos = jnp.concatenate([own_pos, partner_pos], axis=0)
    both_rows = both_q.shape[0]
    cache_code = jnp.where(key_pos_cache < first_pos, -1.0, 1e9).astype(jnp.float32)
    key_code = jnp.concatenate([cache_code, key_pos_slab])[None, :]
    q_code = jnp.broadcast_to(both_pos[:, None], (both_rows, pair_heads)).reshape(-1, 1)
    out, out_max, out_sum = fused_attention(both_q.reshape(-1, HD), q_code, keys, values, key_code)
    summed = out.reshape(both_rows, pair_heads, HD)
    row_max = out_max.reshape(both_rows, pair_heads)
    row_sum = out_sum.reshape(both_rows, pair_heads)

    theirs = jnp.concatenate(
        [summed[slab_rows:].reshape(slab_rows, -1), row_max[slab_rows:], row_sum[slab_rows:]], axis=1
    )
    got = swap(theirs, "row", core_pairs)
    split_at = pair_heads * HD
    other_summed = got[:, :split_at].reshape(slab_rows, pair_heads, HD)
    other_max = got[:, split_at : split_at + pair_heads]
    other_sum = got[:, split_at + pair_heads :]
    mine_max = row_max[:slab_rows]
    top = jnp.maximum(mine_max, other_max)
    scale_mine = jnp.exp(mine_max - top)
    scale_other = jnp.exp(other_max - top)
    numerator = summed[:slab_rows] * scale_mine[..., None] + other_summed * scale_other[..., None]
    denominator = row_sum[:slab_rows] * scale_mine + other_sum * scale_other
    partial = jnp.concatenate([numerator.reshape(slab_rows, -1), top, denominator], axis=1)

    back = lax.all_to_all(partial.reshape(seq_count, tok_rows, -1), "seq", 0, 0, tiled=True)
    back = back.reshape(seq_count // 2, 2, tok_rows, -1)
    half_num = back[..., :split_at].reshape(seq_count // 2, 2, tok_rows, pair_heads, HD)
    half_max = back[..., split_at : split_at + pair_heads]
    half_sum = back[..., split_at + pair_heads :]
    best = jnp.maximum(half_max[:, 0], half_max[:, 1])
    f0 = jnp.exp(half_max[:, 0] - best)
    f1 = jnp.exp(half_max[:, 1] - best)
    num = half_num[:, 0] * f0[..., None] + half_num[:, 1] * f1[..., None]
    den = half_sum[:, 0] * f0 + half_sum[:, 1] * f1
    context = (num / den[..., None]).astype(jnp.bfloat16)
    return context.transpose(1, 0, 2, 3).reshape(tok_rows, -1)


def pl_heads(pair, heads_dev):
    return pair * heads_dev


def solution(mesh):
    in_specs = (
        P(("seq", "row", "col"), None),
        P(("seq", "row", "col"), None),
        P(("seq", "row", "col"), None),
        P(("seq", "row", "col")),
        P(("row", "col"), None),
        P(("row", "col"), None),
        P(),
    )
    out_specs = P(("seq", "row", "col"), None)
    return jax.shard_map(
        on_device, mesh=mesh, in_specs=in_specs, out_specs=out_specs, check_vma=False
    )
```

```python
import math

import numpy as np
import jax
import jax.numpy as jnp
from jax import lax
from jax.sharding import PartitionSpec as P

HQ = 64
KVH = 8
HD = 128

far_position = 1073741824
code_base = 256


def gather_cells(block, cell_axes, cell_count):
    spread = jnp.broadcast_to(block[None], (cell_count,) + block.shape)
    return lax.all_to_all(spread, cell_axes, 0, 0, tiled=True)


def pick_heads(rows, kv_of_peer, tok_rows):
    split = rows.reshape(tok_rows, KVH, 1, HD)
    repeat = kv_of_peer.shape[0] // KVH
    if repeat * KVH == kv_of_peer.shape[0] and np.array_equal(kv_of_peer, np.arange(kv_of_peer.shape[0]) // repeat):
        spread = jnp.broadcast_to(split, (tok_rows, KVH, repeat, HD)).reshape(tok_rows, -1, HD)
    else:
        spread = jnp.take(split[:, :, 0], kv_of_peer, axis=1)
    return spread.transpose(1, 0, 2)


def partner_swap(x, pairs):
    return lax.ppermute(x, "row", pairs)


def partial_attention(query_block, query_pos, keys, values, key_pos_cache, key_pos_slab, cache_rows, first_pos):
    cache_ok = jnp.broadcast_to((key_pos_cache < first_pos)[None, :], (query_pos.shape[0], cache_rows))
    slab_ok = key_pos_slab[None, :] <= query_pos[:, None]
    allowed = jnp.concatenate([cache_ok, slab_ok], axis=1)[:, None, :]
    score_scale = 1.0 / math.sqrt(HD)
    scores = jnp.einsum("thd,nd->thn", query_block, keys, preferred_element_type=jnp.float32) * score_scale
    row_max = jnp.max(jnp.where(allowed, scores, -jnp.inf), axis=-1)
    exponent = jnp.where(allowed, jnp.exp(scores - row_max[..., None]), 0.0)
    row_sum = jnp.sum(exponent, axis=-1)
    summed = jnp.einsum(
        "thn,nd->thd", exponent.astype(jnp.bfloat16), values, preferred_element_type=jnp.float32
    )
    return row_max, row_sum, summed


def swap(x, axes, pairs):
    return lax.ppermute(x, axes, pairs)


def decode(codes):
    codes = codes.astype(jnp.float32)
    return codes[..., 0] * code_base + codes[..., 1]


def on_device(queries, new_keys, new_values, positions, cache_keys, cache_values, slab_start):
    seq_count = lax.axis_size("seq")
    cell_axes = ("row", "col")
    row_count = lax.axis_size("row")
    col_count = lax.axis_size("col")
    cell_count = row_count * col_count
    heads_dev = HQ // seq_count
    group_size = HQ // KVH
    tok_rows = queries.shape[0]
    first_pos = slab_start[0]
    seq_index = lax.axis_index("seq")
    kv_first = seq_index * heads_dev // group_size
    parity = seq_index % 2
    core = lax.axis_index("row") % 2
    quarter = parity * 2 + core
    core_pairs = [(r, r ^ 1) for r in range(row_count)]
    seq_pairs = [(q, q ^ 1) for q in range(seq_count)]
    diag_pairs = [(q * row_count + r, (q ^ 1) * row_count + (r ^ 1)) for q in range(seq_count) for r in range(row_count)]
    width = 2 * HD
    pair_heads = 2 * heads_dev
    half_tok = tok_rows // 2

    q_pairs = queries.reshape(tok_rows, seq_count // 2, 1, pair_heads * HD)
    q_part = jnp.broadcast_to(q_pairs, (tok_rows, seq_count // 2, 2, pair_heads * HD)).reshape(tok_rows, seq_count, -1)
    kv_local = jnp.concatenate(
        [new_keys.reshape(tok_rows, KVH, 1, HD), new_values.reshape(tok_rows, KVH, 1, HD)], axis=2
    ).reshape(2, half_tok, KVH, 1, width)
    repeat = seq_count // (2 * KVH)
    kv_part = jnp.broadcast_to(
        kv_local.transpose(2, 3, 0, 1, 4)[:, :, None], (KVH, 1, repeat, 2, half_tok, width)
    ).reshape(seq_count, half_tok * width)
    codes = jnp.stack([positions // code_base, positions % code_base], axis=1).astype(jnp.bfloat16)
    codes = jnp.pad(codes.reshape(1, tok_rows * 2), ((0, 0), (0, 128 - tok_rows * 2)))
    send = jnp.concatenate(
        [q_part.transpose(1, 0, 2).reshape(seq_count, -1), kv_part, jnp.broadcast_to(codes, (seq_count, 128))],
        axis=1,
    )
    recv = lax.all_to_all(send, "seq", 0, 0, tiled=True)
    q_len = tok_rows * pair_heads * HD
    kvp_len = half_tok * width
    slab_rows = seq_count * tok_rows
    query_block = recv[:, :q_len].reshape(slab_rows, pair_heads, HD)
    slab_kv = recv[:, q_len : q_len + kvp_len].reshape(seq_count * half_tok, width)
    got_codes = recv[:, q_len + kvp_len : q_len + kvp_len + tok_rows * 2].reshape(seq_count, tok_rows, 2)
    own_pos = decode(got_codes.reshape(slab_rows, 2))
    slab_codes = lax.dynamic_slice_in_dim(got_codes, parity * half_tok, half_tok, 1).reshape(seq_count * half_tok, 2)

    partner_q = swap(
        jnp.concatenate([query_block.reshape(slab_rows, -1), got_codes.reshape(slab_rows, 2)], axis=1), "row", core_pairs
    )
    partner_block = partner_q[:, : pair_heads * HD].reshape(slab_rows, pair_heads, HD)
    partner_pos = decode(partner_q[:, pair_heads * HD :])

    cache_block = jnp.concatenate(
        [
            lax.dynamic_slice_in_dim(cache_keys, kv_first * HD, HD, 1),
            lax.dynamic_slice_in_dim(cache_values, kv_first * HD, HD, 1),
        ],
        axis=1,
    )
    cache_len = cache_block.shape[0]
    part_cache = cache_len // 4
    half_slab = slab_kv.shape[0] // 2
    code_rows = jnp.pad(slab_codes.reshape(2, half_slab * 2), ((0, 0), (0, width - half_slab * 2)))
    cache_pair = lax.dynamic_slice_in_dim(cache_block, parity * 2 * part_cache, 2 * part_cache, 0)
    halves = jnp.stack(
        [
            jnp.concatenate(
                [
                    cache_pair[b * part_cache : (b + 1) * part_cache],
                    slab_kv[b * half_slab : (b + 1) * half_slab],
                    code_rows[b : b + 1],
                ],
                axis=0,
            )
            for b in range(2)
        ]
    )
    per_dest = jnp.broadcast_to(
        halves[None, :, None], (row_count // 2, 2, col_count) + halves.shape[1:]
    ).reshape((cell_count,) + halves.shape[1:])
    every = lax.all_to_all(per_dest, cell_axes, 0, 0, tiled=True)
    cache_got = every[:, :part_cache].reshape(-1, width)
    slab_got = every[:, part_cache : part_cache + half_slab].reshape(-1, width)
    key_pos_slab = decode(every[:, part_cache + half_slab, : 2 * half_slab].reshape(-1, 2))
    key_pos_cache = (
        jnp.arange(cell_count, dtype=jnp.int32)[:, None] * cache_len
        + quarter * part_cache
        + jnp.arange(part_cache, dtype=jnp.int32)[None, :]
    ).reshape(-1)
    keys = jnp.concatenate([cache_got[:, :HD], slab_got[:, :HD]], axis=0)
    values = jnp.concatenate([cache_got[:, HD:], slab_got[:, HD:]], axis=0)

    both_q = jnp.concatenate([query_block, partner_block], axis=0)
    both_pos = jnp.concatenate([own_pos, partner_pos], axis=0)
    row_max, row_sum, summed = partial_attention(
        both_q, both_pos, keys, values, key_pos_cache, key_pos_slab, cache_got.shape[0], first_pos
    )

    theirs = jnp.concatenate(
        [summed[slab_rows:].reshape(slab_rows, -1), row_max[slab_rows:], row_sum[slab_rows:]], axis=1
    )
    got = swap(theirs, "row", core_pairs)
    split_at = pair_heads * HD
    other_summed = got[:, :split_at].reshape(slab_rows, pair_heads, HD)
    other_max = got[:, split_at : split_at + pair_heads]
    other_sum = got[:, split_at + pair_heads :]
    mine_max = row_max[:slab_rows]
    top = jnp.maximum(mine_max, other_max)
    scale_mine = jnp.exp(mine_max - top)
    scale_other = jnp.exp(other_max - top)
    numerator = summed[:slab_rows] * scale_mine[..., None] + other_summed * scale_other[..., None]
    denominator = row_sum[:slab_rows] * scale_mine + other_sum * scale_other
    normed = (numerator / denominator[..., None]).astype(jnp.bfloat16).reshape(slab_rows, -1)
    log_weight = top + jnp.log(denominator)
    pieces = []
    rest = log_weight
    for _ in range(3):
        piece = lax.reduce_precision(rest, exponent_bits=8, mantissa_bits=7)
        pieces.append(piece.astype(jnp.bfloat16))
        rest = rest - piece
    coded = jnp.stack(pieces, axis=1).reshape(slab_rows, -1)
    code_width = 128 * pl_cdiv(coded.shape[1], 128)
    coded = jnp.pad(coded, ((0, 0), (0, code_width - coded.shape[1])))
    partial = jnp.concatenate([normed, coded], axis=1)

    back = lax.all_to_all(partial.reshape(seq_count, tok_rows, -1), "seq", 0, 0, tiled=True)
    back = back.reshape(seq_count // 2, 2, tok_rows, -1)
    half_num = back[..., :split_at].astype(jnp.float32).reshape(seq_count // 2, 2, tok_rows, pair_heads, HD)
    half_log = (
        back[..., split_at : split_at + 3 * pair_heads]
        .astype(jnp.float32)
        .reshape(seq_count // 2, 2, tok_rows, 3, pair_heads)
        .sum(axis=3)
    )
    best = jnp.maximum(half_log[:, 0], half_log[:, 1])
    w0 = jnp.exp(half_log[:, 0] - best)
    w1 = jnp.exp(half_log[:, 1] - best)
    num = half_num[:, 0] * w0[..., None] + half_num[:, 1] * w1[..., None]
    context = (num / (w0 + w1)[..., None]).astype(jnp.bfloat16)
    return context.transpose(1, 0, 2, 3).reshape(tok_rows, -1)


def pl_cdiv(a, b):
    return (a + b - 1) // b


def pl_heads(pair, heads_dev):
    return pair * heads_dev


def solution(mesh):
    in_specs = (
        P(("seq", "row", "col"), None),
        P(("seq", "row", "col"), None),
        P(("seq", "row", "col"), None),
        P(("seq", "row", "col")),
        P(("row", "col"), None),
        P(("row", "col"), None),
        P(),
    )
    out_specs = P(("seq", "row", "col"), None)
    return jax.shard_map(
        on_device, mesh=mesh, in_specs=in_specs, out_specs=out_specs, check_vma=False
    )
```

```python
import math

import numpy as np
import jax
import jax.numpy as jnp
from jax import lax
from jax.sharding import PartitionSpec as P

HQ = 64
KVH = 8
HD = 128

far_position = 1073741824
code_base = 256


def gather_cells(block, cell_axes, cell_count):
    spread = jnp.broadcast_to(block[None], (cell_count,) + block.shape)
    return lax.all_to_all(spread, cell_axes, 0, 0, tiled=True)


def pick_heads(rows, kv_of_peer, tok_rows):
    split = rows.reshape(tok_rows, KVH, 1, HD)
    repeat = kv_of_peer.shape[0] // KVH
    if repeat * KVH == kv_of_peer.shape[0] and np.array_equal(kv_of_peer, np.arange(kv_of_peer.shape[0]) // repeat):
        spread = jnp.broadcast_to(split, (tok_rows, KVH, repeat, HD)).reshape(tok_rows, -1, HD)
    else:
        spread = jnp.take(split[:, :, 0], kv_of_peer, axis=1)
    return spread.transpose(1, 0, 2)


def partner_swap(x, pairs):
    return lax.ppermute(x, "row", pairs)


def partial_attention(query_block, query_pos, keys, values, key_pos_cache, key_pos_slab, cache_rows, first_pos):
    cache_ok = jnp.broadcast_to((key_pos_cache < first_pos)[None, :], (query_pos.shape[0], cache_rows))
    slab_ok = key_pos_slab[None, :] <= query_pos[:, None]
    allowed = jnp.concatenate([cache_ok, slab_ok], axis=1)[:, None, :]
    score_scale = 1.0 / math.sqrt(HD)
    scores = jnp.einsum("thd,nd->thn", query_block, keys, preferred_element_type=jnp.float32) * score_scale
    row_max = jnp.max(jnp.where(allowed, scores, -jnp.inf), axis=-1)
    exponent = jnp.where(allowed, jnp.exp(scores - row_max[..., None]), 0.0)
    row_sum = jnp.sum(exponent, axis=-1)
    summed = jnp.einsum(
        "thn,nd->thd", exponent.astype(jnp.bfloat16), values, preferred_element_type=jnp.float32
    )
    return row_max, row_sum, summed


def swap(x, axes, pairs):
    return lax.ppermute(x, axes, pairs)


def decode(codes):
    codes = codes.astype(jnp.float32)
    return codes[..., 0] * code_base + codes[..., 1]


def on_device(queries, new_keys, new_values, positions, cache_keys, cache_values, slab_start):
    seq_count = lax.axis_size("seq")
    cell_axes = ("row", "col")
    row_count = lax.axis_size("row")
    col_count = lax.axis_size("col")
    cell_count = row_count * col_count
    heads_dev = HQ // seq_count
    group_size = HQ // KVH
    tok_rows = queries.shape[0]
    first_pos = slab_start[0]
    seq_index = lax.axis_index("seq")
    kv_first = seq_index * heads_dev // group_size
    quad = group_size // heads_dev
    quads = seq_count // quad
    u = seq_index % quad
    core = lax.axis_index("row") % 2
    part = u * 2 + core
    parts = quad * 2
    core_pairs = [(r, r ^ 1) for r in range(row_count)]
    width = 2 * HD
    quad_heads = group_size

    q_quads = queries.reshape(tok_rows, quads, 1, quad_heads * HD)
    q_part = jnp.broadcast_to(q_quads, (tok_rows, quads, quad, quad_heads * HD)).reshape(tok_rows, seq_count, -1)
    kv_local = jnp.concatenate(
        [new_keys.reshape(tok_rows, KVH, HD), new_values.reshape(tok_rows, KVH, HD)], axis=2
    )
    kv_part = kv_local.transpose(1, 0, 2).reshape(seq_count, width)
    codes = jnp.stack([positions // code_base, positions % code_base], axis=1).astype(jnp.bfloat16)
    codes = jnp.pad(codes.reshape(1, tok_rows * 2), ((0, 0), (0, 128 - tok_rows * 2)))
    send = jnp.concatenate(
        [q_part.transpose(1, 0, 2).reshape(seq_count, -1), kv_part, jnp.broadcast_to(codes, (seq_count, 128))],
        axis=1,
    )
    recv = lax.all_to_all(send, "seq", 0, 0, tiled=True)
    q_len = tok_rows * quad_heads * HD
    slab_rows = seq_count * tok_rows
    query_block = recv[:, :q_len].reshape(slab_rows, quad_heads, HD)
    slab_kv = recv[:, q_len : q_len + width]
    got_codes = recv[:, q_len + width : q_len + width + tok_rows * 2].reshape(seq_count, tok_rows, 2)
    own_pos = decode(got_codes.reshape(slab_rows, 2))
    slab_codes = lax.dynamic_index_in_dim(got_codes, u, 1, keepdims=False)

    partner_q = swap(
        jnp.concatenate([query_block.reshape(slab_rows, -1), got_codes.reshape(slab_rows, 2)], axis=1), "row", core_pairs
    )
    partner_block = partner_q[:, : quad_heads * HD].reshape(slab_rows, quad_heads, HD)
    partner_pos = decode(partner_q[:, quad_heads * HD :])

    cache_block = jnp.concatenate(
        [
            lax.dynamic_slice_in_dim(cache_keys, kv_first * HD, HD, 1),
            lax.dynamic_slice_in_dim(cache_values, kv_first * HD, HD, 1),
        ],
        axis=1,
    )
    cache_len = cache_block.shape[0]
    part_cache = cache_len // parts
    half_slab = seq_count // 2
    code_rows = jnp.pad(slab_codes.reshape(2, half_slab * 2), ((0, 0), (0, width - half_slab * 2)))
    cache_pair = lax.dynamic_slice_in_dim(cache_block, u * 2 * part_cache, 2 * part_cache, 0)
    halves = jnp.stack(
        [
            jnp.concatenate(
                [
                    cache_pair[b * part_cache : (b + 1) * part_cache],
                    slab_kv[b * half_slab : (b + 1) * half_slab],
                    code_rows[b : b + 1],
                ],
                axis=0,
            )
            for b in range(2)
        ]
    )
    per_dest = jnp.broadcast_to(
        halves[None, :, None], (row_count // 2, 2, col_count) + halves.shape[1:]
    ).reshape((cell_count,) + halves.shape[1:])
    every = lax.all_to_all(per_dest, cell_axes, 0, 0, tiled=True)
    cache_got = every[:, :part_cache].reshape(-1, width)
    slab_got = every[:, part_cache : part_cache + half_slab].reshape(-1, width)
    key_pos_slab = decode(every[:, part_cache + half_slab, : 2 * half_slab].reshape(-1, 2))
    key_pos_cache = (
        jnp.arange(cell_count, dtype=jnp.int32)[:, None] * cache_len
        + part * part_cache
        + jnp.arange(part_cache, dtype=jnp.int32)[None, :]
    ).reshape(-1)
    keys = jnp.concatenate([cache_got[:, :HD], slab_got[:, :HD]], axis=0)
    values = jnp.concatenate([cache_got[:, HD:], slab_got[:, HD:]], axis=0)

    both_q = jnp.concatenate([query_block, partner_block], axis=0)
    both_pos = jnp.concatenate([own_pos, partner_pos], axis=0)
    row_max, row_sum, summed = partial_attention(
        both_q, both_pos, keys, values, key_pos_cache, key_pos_slab, cache_got.shape[0], first_pos
    )

    theirs = jnp.concatenate(
        [summed[slab_rows:].reshape(slab_rows, -1), row_max[slab_rows:], row_sum[slab_rows:]], axis=1
    )
    got = swap(theirs, "row", core_pairs)
    split_at = quad_heads * HD
    other_summed = got[:, :split_at].reshape(slab_rows, quad_heads, HD)
    other_max = got[:, split_at : split_at + quad_heads]
    other_sum = got[:, split_at + quad_heads :]
    mine_max = row_max[:slab_rows]
    top = jnp.maximum(mine_max, other_max)
    scale_mine = jnp.exp(mine_max - top)
    scale_other = jnp.exp(other_max - top)
    numerator = summed[:slab_rows] * scale_mine[..., None] + other_summed * scale_other[..., None]
    denominator = row_sum[:slab_rows] * scale_mine + other_sum * scale_other

    normed = (numerator / denominator[..., None]).astype(jnp.bfloat16).reshape(slab_rows, -1)
    log_weight = top + jnp.log(denominator)
    pieces = []
    rest = log_weight
    for _ in range(3):
        piece = lax.reduce_precision(rest, exponent_bits=8, mantissa_bits=7)
        pieces.append(piece.astype(jnp.bfloat16))
        rest = rest - piece
    coded = jnp.stack(pieces, axis=1).reshape(slab_rows, -1)
    code_width = 128 * pl_cdiv(coded.shape[1], 128)
    coded = jnp.pad(coded, ((0, 0), (0, code_width - coded.shape[1])))
    partial = jnp.concatenate([normed, coded], axis=1)

    back = lax.all_to_all(partial.reshape(seq_count, tok_rows, -1), "seq", 0, 0, tiled=True)
    back = back.reshape(quads, quad, tok_rows, -1)
    part_num = back[..., :split_at].astype(jnp.float32).reshape(quads, quad, tok_rows, quad_heads, HD)
    part_log = (
        back[..., split_at : split_at + 3 * quad_heads]
        .astype(jnp.float32)
        .reshape(quads, quad, tok_rows, 3, quad_heads)
        .sum(axis=3)
    )
    best = jnp.max(part_log, axis=1, keepdims=True)
    weight = jnp.exp(part_log - best)
    num = jnp.sum(part_num * weight[..., None], axis=1)
    context = (num / jnp.sum(weight, axis=1)[..., None]).astype(jnp.bfloat16)
    return context.transpose(1, 0, 2, 3).reshape(tok_rows, -1)


def pl_cdiv(a, b):
    return (a + b - 1) // b


def pl_heads(pair, heads_dev):
    return pair * heads_dev


def solution(mesh):
    in_specs = (
        P(("seq", "row", "col"), None),
        P(("seq", "row", "col"), None),
        P(("seq", "row", "col"), None),
        P(("seq", "row", "col")),
        P(("row", "col"), None),
        P(("row", "col"), None),
        P(),
    )
    out_specs = P(("seq", "row", "col"), None)
    return jax.shard_map(
        on_device, mesh=mesh, in_specs=in_specs, out_specs=out_specs, check_vma=False
    )
```

```python
import math

import numpy as np
import jax
import jax.numpy as jnp
from jax import lax
from jax.sharding import PartitionSpec as P

HQ = 64
KVH = 8
HD = 128

far_position = 1073741824
code_base = 256


def gather_cells(block, cell_axes, cell_count):
    spread = jnp.broadcast_to(block[None], (cell_count,) + block.shape)
    return lax.all_to_all(spread, cell_axes, 0, 0, tiled=True)


def pick_heads(rows, kv_of_peer, tok_rows):
    split = rows.reshape(tok_rows, KVH, 1, HD)
    repeat = kv_of_peer.shape[0] // KVH
    if repeat * KVH == kv_of_peer.shape[0] and np.array_equal(kv_of_peer, np.arange(kv_of_peer.shape[0]) // repeat):
        spread = jnp.broadcast_to(split, (tok_rows, KVH, repeat, HD)).reshape(tok_rows, -1, HD)
    else:
        spread = jnp.take(split[:, :, 0], kv_of_peer, axis=1)
    return spread.transpose(1, 0, 2)


def partner_swap(x, pairs):
    return lax.ppermute(x, "row", pairs)


def partial_attention(query_block, query_pos, keys, values, key_pos_cache, key_pos_slab, cache_rows, first_pos):
    cache_ok = jnp.broadcast_to((key_pos_cache < first_pos)[None, :], (query_pos.shape[0], cache_rows))
    slab_ok = key_pos_slab[None, :] <= query_pos[:, None]
    allowed = jnp.concatenate([cache_ok, slab_ok], axis=1)[:, None, :]
    score_scale = 1.0 / math.sqrt(HD)
    scores = jnp.einsum("thd,nd->thn", query_block, keys, preferred_element_type=jnp.float32) * score_scale
    row_max = jnp.max(jnp.where(allowed, scores, -jnp.inf), axis=-1)
    exponent = jnp.where(allowed, jnp.exp(scores - row_max[..., None]), 0.0)
    row_sum = jnp.sum(exponent, axis=-1)
    summed = jnp.einsum(
        "thn,nd->thd", exponent.astype(jnp.bfloat16), values, preferred_element_type=jnp.float32
    )
    return row_max, row_sum, summed


def swap(x, axes, pairs):
    return lax.ppermute(x, axes, pairs)


def decode(codes):
    codes = codes.astype(jnp.float32)
    return codes[..., 0] * code_base + codes[..., 1]


def coded_partial(normed, log_weight):
    rows = normed.shape[0]
    pieces = []
    rest = log_weight
    for _ in range(3):
        piece = lax.reduce_precision(rest, exponent_bits=8, mantissa_bits=7)
        pieces.append(piece.astype(jnp.bfloat16))
        rest = rest - piece
    coded = jnp.stack(pieces, axis=1).reshape(rows, -1)
    code_width = 128 * pl_cdiv(coded.shape[1], 128)
    coded = jnp.pad(coded, ((0, 0), (0, code_width - coded.shape[1])))
    return jnp.concatenate([normed.astype(jnp.bfloat16).reshape(rows, -1), coded], axis=1)


def decode_partial(packed, heads):
    rows = packed.shape[0]
    split_at = heads * HD
    normed = packed[:, :split_at].astype(jnp.float32).reshape(rows, heads, HD)
    log_weight = packed[:, split_at : split_at + 3 * heads].astype(jnp.float32).reshape(rows, 3, heads).sum(axis=1)
    return normed, log_weight


def on_device(queries, new_keys, new_values, positions, cache_keys, cache_values, slab_start):
    seq_count = lax.axis_size("seq")
    cell_axes = ("row", "col")
    row_count = lax.axis_size("row")
    col_count = lax.axis_size("col")
    cell_count = row_count * col_count
    heads_dev = HQ // seq_count
    group_size = HQ // KVH
    tok_rows = queries.shape[0]
    first_pos = slab_start[0]
    seq_index = lax.axis_index("seq")
    kv_first = seq_index * heads_dev // group_size
    quad = group_size // heads_dev
    quads = seq_count // quad
    u = seq_index % quad
    core = lax.axis_index("row") % 2
    part = u * 2 + core
    parts = quad * 2
    core_pairs = [(r, r ^ 1) for r in range(row_count)]
    width = 2 * HD
    quad_heads = group_size

    q_quads = queries.reshape(tok_rows, quads, 1, quad_heads * HD)
    q_part = jnp.broadcast_to(q_quads, (tok_rows, quads, quad, quad_heads * HD)).reshape(tok_rows, seq_count, -1)
    kv_local = jnp.concatenate(
        [new_keys.reshape(tok_rows, KVH, HD), new_values.reshape(tok_rows, KVH, HD)], axis=2
    )
    kv_part = kv_local.transpose(1, 0, 2).reshape(seq_count, width)
    codes = jnp.stack([positions // code_base, positions % code_base], axis=1).astype(jnp.bfloat16)
    codes = jnp.pad(codes.reshape(1, tok_rows * 2), ((0, 0), (0, 128 - tok_rows * 2)))
    send = jnp.concatenate(
        [q_part.transpose(1, 0, 2).reshape(seq_count, -1), kv_part, jnp.broadcast_to(codes, (seq_count, 128))],
        axis=1,
    )
    recv = lax.all_to_all(send, "seq", 0, 0, tiled=True)
    q_len = tok_rows * quad_heads * HD
    slab_rows = seq_count * tok_rows
    query_block = recv[:, :q_len].reshape(slab_rows, quad_heads, HD)
    slab_kv = recv[:, q_len : q_len + width]
    got_codes = recv[:, q_len + width : q_len + width + tok_rows * 2].reshape(seq_count, tok_rows, 2)
    own_pos = decode(got_codes.reshape(slab_rows, 2))
    slab_codes = lax.dynamic_index_in_dim(got_codes, u, 1, keepdims=False)

    partner_q = swap(
        jnp.concatenate([query_block.reshape(slab_rows, -1), got_codes.reshape(slab_rows, 2)], axis=1), "row", core_pairs
    )
    partner_block = partner_q[:, : quad_heads * HD].reshape(slab_rows, quad_heads, HD)
    partner_pos = decode(partner_q[:, quad_heads * HD :])

    cache_block = jnp.concatenate(
        [
            lax.dynamic_slice_in_dim(cache_keys, kv_first * HD, HD, 1),
            lax.dynamic_slice_in_dim(cache_values, kv_first * HD, HD, 1),
        ],
        axis=1,
    )
    cache_len = cache_block.shape[0]
    part_cache = cache_len // parts
    half_slab = seq_count // 2
    code_rows = jnp.pad(slab_codes.reshape(2, half_slab * 2), ((0, 0), (0, width - half_slab * 2)))
    cache_pair = lax.dynamic_slice_in_dim(cache_block, u * 2 * part_cache, 2 * part_cache, 0)
    halves = jnp.stack(
        [
            jnp.concatenate(
                [
                    cache_pair[b * part_cache : (b + 1) * part_cache],
                    slab_kv[b * half_slab : (b + 1) * half_slab],
                    code_rows[b : b + 1],
                ],
                axis=0,
            )
            for b in range(2)
        ]
    )
    per_dest = jnp.broadcast_to(
        halves[None, :, None], (row_count // 2, 2, col_count) + halves.shape[1:]
    ).reshape((cell_count,) + halves.shape[1:])
    every = lax.all_to_all(per_dest, cell_axes, 0, 0, tiled=True)
    cache_got = every[:, :part_cache].reshape(-1, width)
    slab_got = every[:, part_cache : part_cache + half_slab].reshape(-1, width)
    key_pos_slab = decode(every[:, part_cache + half_slab, : 2 * half_slab].reshape(-1, 2))
    key_pos_cache = (
        jnp.arange(cell_count, dtype=jnp.int32)[:, None] * cache_len
        + part * part_cache
        + jnp.arange(part_cache, dtype=jnp.int32)[None, :]
    ).reshape(-1)
    keys = jnp.concatenate([cache_got[:, :HD], slab_got[:, :HD]], axis=0)
    values = jnp.concatenate([cache_got[:, HD:], slab_got[:, HD:]], axis=0)

    both_q = jnp.concatenate([query_block, partner_block], axis=0)
    both_pos = jnp.concatenate([own_pos, partner_pos], axis=0)
    row_max, row_sum, summed = partial_attention(
        both_q, both_pos, keys, values, key_pos_cache, key_pos_slab, cache_got.shape[0], first_pos
    )

    log_all = row_max + jnp.log(row_sum)
    normed_all = summed / row_sum[..., None]
    theirs = coded_partial(normed_all[slab_rows:], log_all[slab_rows:])
    other_normed, other_log = decode_partial(swap(theirs, "row", core_pairs), quad_heads)
    mine_log = log_all[:slab_rows]
    top = jnp.maximum(mine_log, other_log)
    w_mine = jnp.exp(mine_log - top)
    w_other = jnp.exp(other_log - top)
    total = w_mine + w_other
    combined = (normed_all[:slab_rows] * w_mine[..., None] + other_normed * w_other[..., None]) / total[..., None]
    partial = coded_partial(combined, top + jnp.log(total))
    split_at = quad_heads * HD

    back = lax.all_to_all(partial.reshape(seq_count, tok_rows, -1), "seq", 0, 0, tiled=True)
    back = back.reshape(quads, quad, tok_rows, -1)
    part_num = back[..., :split_at].astype(jnp.float32).reshape(quads, quad, tok_rows, quad_heads, HD)
    part_log = (
        back[..., split_at : split_at + 3 * quad_heads]
        .astype(jnp.float32)
        .reshape(quads, quad, tok_rows, 3, quad_heads)
        .sum(axis=3)
    )
    best = jnp.max(part_log, axis=1, keepdims=True)
    weight = jnp.exp(part_log - best)
    num = jnp.sum(part_num * weight[..., None], axis=1)
    context = (num / jnp.sum(weight, axis=1)[..., None]).astype(jnp.bfloat16)
    return context.transpose(1, 0, 2, 3).reshape(tok_rows, -1)


def pl_cdiv(a, b):
    return (a + b - 1) // b


def pl_heads(pair, heads_dev):
    return pair * heads_dev


def solution(mesh):
    in_specs = (
        P(("seq", "row", "col"), None),
        P(("seq", "row", "col"), None),
        P(("seq", "row", "col"), None),
        P(("seq", "row", "col")),
        P(("row", "col"), None),
        P(("row", "col"), None),
        P(),
    )
    out_specs = P(("seq", "row", "col"), None)
    return jax.shard_map(
        on_device, mesh=mesh, in_specs=in_specs, out_specs=out_specs, check_vma=False
    )
```

```python
import math

import numpy as np
import jax
import jax.numpy as jnp
from jax import lax
from jax.sharding import PartitionSpec as P

HQ = 64
KVH = 8
HD = 128

far_position = 1073741824
code_base = 256


def gather_cells(block, cell_axes, cell_count):
    spread = jnp.broadcast_to(block[None], (cell_count,) + block.shape)
    return lax.all_to_all(spread, cell_axes, 0, 0, tiled=True)


def pick_heads(rows, kv_of_peer, tok_rows):
    split = rows.reshape(tok_rows, KVH, 1, HD)
    repeat = kv_of_peer.shape[0] // KVH
    if repeat * KVH == kv_of_peer.shape[0] and np.array_equal(kv_of_peer, np.arange(kv_of_peer.shape[0]) // repeat):
        spread = jnp.broadcast_to(split, (tok_rows, KVH, repeat, HD)).reshape(tok_rows, -1, HD)
    else:
        spread = jnp.take(split[:, :, 0], kv_of_peer, axis=1)
    return spread.transpose(1, 0, 2)


def partner_swap(x, pairs):
    return lax.ppermute(x, "row", pairs)


def partial_attention(query_block, query_pos, keys, values, key_pos_cache, key_pos_slab, cache_rows, first_pos):
    cache_ok = jnp.broadcast_to((key_pos_cache < first_pos)[None, :], (query_pos.shape[0], cache_rows))
    slab_ok = key_pos_slab[None, :] <= query_pos[:, None]
    allowed = jnp.concatenate([cache_ok, slab_ok], axis=1)[:, None, :]
    score_scale = 1.0 / math.sqrt(HD)
    scores = jnp.einsum("thd,nd->thn", query_block, keys, preferred_element_type=jnp.float32) * score_scale
    row_max = jnp.max(jnp.where(allowed, scores, -jnp.inf), axis=-1)
    exponent = jnp.where(allowed, jnp.exp(scores - row_max[..., None]), 0.0)
    row_sum = jnp.sum(exponent, axis=-1)
    summed = jnp.einsum(
        "thn,nd->thd", exponent.astype(jnp.bfloat16), values, preferred_element_type=jnp.float32
    )
    return row_max, row_sum, summed


def swap(x, axes, pairs):
    return lax.ppermute(x, axes, pairs)


def decode(codes):
    codes = codes.astype(jnp.float32)
    return codes[..., 0] * code_base + codes[..., 1]


def coded_partial(normed, log_weight):
    rows = normed.shape[0]
    pieces = []
    rest = log_weight
    for _ in range(3):
        piece = lax.reduce_precision(rest, exponent_bits=8, mantissa_bits=7)
        pieces.append(piece.astype(jnp.bfloat16))
        rest = rest - piece
    coded = jnp.stack(pieces, axis=1).reshape(rows, -1)
    code_width = 128 * pl_cdiv(coded.shape[1], 128)
    coded = jnp.pad(coded, ((0, 0), (0, code_width - coded.shape[1])))
    return jnp.concatenate([normed.astype(jnp.bfloat16).reshape(rows, -1), coded], axis=1)


def decode_partial(packed, heads):
    rows = packed.shape[0]
    split_at = heads * HD
    normed = packed[:, :split_at].astype(jnp.float32).reshape(rows, heads, HD)
    log_weight = packed[:, split_at : split_at + 3 * heads].astype(jnp.float32).reshape(rows, 3, heads).sum(axis=1)
    return normed, log_weight


def on_device(queries, new_keys, new_values, positions, cache_keys, cache_values, slab_start):
    seq_count = lax.axis_size("seq")
    cell_axes = ("row", "col")
    row_count = lax.axis_size("row")
    col_count = lax.axis_size("col")
    cell_count = row_count * col_count
    heads_dev = HQ // seq_count
    group_size = HQ // KVH
    tok_rows = queries.shape[0]
    first_pos = slab_start[0]
    seq_index = lax.axis_index("seq")
    kv_first = seq_index * heads_dev // group_size
    quad = group_size // heads_dev
    quads = seq_count // quad
    u = seq_index % quad
    width = 2 * HD
    quad_heads = group_size

    q_quads = queries.reshape(tok_rows, quads, 1, quad_heads * HD)
    q_part = jnp.broadcast_to(q_quads, (tok_rows, quads, quad, quad_heads * HD)).reshape(tok_rows, seq_count, -1)
    kv_local = jnp.concatenate(
        [new_keys.reshape(tok_rows, KVH, HD), new_values.reshape(tok_rows, KVH, HD)], axis=2
    )
    kv_part = kv_local.transpose(1, 0, 2).reshape(seq_count, width)
    codes = jnp.stack([positions // code_base, positions % code_base], axis=1).astype(jnp.bfloat16)
    codes = jnp.pad(codes.reshape(1, tok_rows * 2), ((0, 0), (0, 128 - tok_rows * 2)))
    send = jnp.concatenate(
        [q_part.transpose(1, 0, 2).reshape(seq_count, -1), kv_part, jnp.broadcast_to(codes, (seq_count, 128))],
        axis=1,
    )
    recv = lax.all_to_all(send, "seq", 0, 0, tiled=True)
    q_len = tok_rows * quad_heads * HD
    slab_rows = seq_count * tok_rows
    query_block = recv[:, :q_len].reshape(slab_rows, quad_heads, HD)
    slab_kv = recv[:, q_len : q_len + width]
    got_codes = recv[:, q_len + width : q_len + width + tok_rows * 2].reshape(seq_count, tok_rows, 2)
    own_pos = decode(got_codes.reshape(slab_rows, 2))
    slab_codes = lax.dynamic_index_in_dim(got_codes, u, 1, keepdims=False)

    cache_block = jnp.concatenate(
        [
            lax.dynamic_slice_in_dim(cache_keys, kv_first * HD, HD, 1),
            lax.dynamic_slice_in_dim(cache_values, kv_first * HD, HD, 1),
        ],
        axis=1,
    )
    cache_len = cache_block.shape[0]
    part_cache = cache_len // quad
    code_row = jnp.pad(slab_codes.reshape(1, seq_count * 2), ((0, 0), (0, width - seq_count * 2)))
    block = jnp.concatenate(
        [lax.dynamic_slice_in_dim(cache_block, u * part_cache, part_cache, 0), slab_kv, code_row], axis=0
    )
    every = gather_cells(block, cell_axes, cell_count)
    cache_got = every[:, :part_cache].reshape(-1, width)
    slab_got = every[:, part_cache : part_cache + seq_count].reshape(-1, width)
    key_pos_slab = decode(every[:, part_cache + seq_count, : 2 * seq_count].reshape(-1, 2))
    key_pos_cache = (
        jnp.arange(cell_count, dtype=jnp.int32)[:, None] * cache_len
        + u * part_cache
        + jnp.arange(part_cache, dtype=jnp.int32)[None, :]
    ).reshape(-1)
    keys = jnp.concatenate([cache_got[:, :HD], slab_got[:, :HD]], axis=0)
    values = jnp.concatenate([cache_got[:, HD:], slab_got[:, HD:]], axis=0)

    row_max, row_sum, summed = partial_attention(
        query_block, own_pos, keys, values, key_pos_cache, key_pos_slab, cache_got.shape[0], first_pos
    )
    partial = coded_partial(summed / row_sum[..., None], row_max + jnp.log(row_sum))
    split_at = quad_heads * HD

    back = lax.all_to_all(partial.reshape(seq_count, tok_rows, -1), "seq", 0, 0, tiled=True)
    back = back.reshape(quads, quad, tok_rows, -1)
    part_num = back[..., :split_at].astype(jnp.float32).reshape(quads, quad, tok_rows, quad_heads, HD)
    part_log = (
        back[..., split_at : split_at + 3 * quad_heads]
        .astype(jnp.float32)
        .reshape(quads, quad, tok_rows, 3, quad_heads)
        .sum(axis=3)
    )
    best = jnp.max(part_log, axis=1, keepdims=True)
    weight = jnp.exp(part_log - best)
    num = jnp.sum(part_num * weight[..., None], axis=1)
    context = (num / jnp.sum(weight, axis=1)[..., None]).astype(jnp.bfloat16)
    return context.transpose(1, 0, 2, 3).reshape(tok_rows, -1)


def pl_cdiv(a, b):
    return (a + b - 1) // b


def pl_heads(pair, heads_dev):
    return pair * heads_dev


def solution(mesh):
    in_specs = (
        P(("seq", "row", "col"), None),
        P(("seq", "row", "col"), None),
        P(("seq", "row", "col"), None),
        P(("seq", "row", "col")),
        P(("row", "col"), None),
        P(("row", "col"), None),
        P(),
    )
    out_specs = P(("seq", "row", "col"), None)
    return jax.shard_map(
        on_device, mesh=mesh, in_specs=in_specs, out_specs=out_specs, check_vma=False
    )
```

```python
import math

import numpy as np
import jax
import jax.numpy as jnp
from jax import lax
from jax.sharding import PartitionSpec as P
from jax.experimental import pallas as pl
from jax.experimental.pallas import tpu as pltpu

HQ = 64
KVH = 8
HD = 128

far_position = 1073741824
code_base = 256


def gather_cells(block, cell_axes, cell_count):
    spread = jnp.broadcast_to(block[None], (cell_count,) + block.shape)
    return lax.all_to_all(spread, cell_axes, 0, 0, tiled=True)


def pick_heads(rows, kv_of_peer, tok_rows):
    split = rows.reshape(tok_rows, KVH, 1, HD)
    repeat = kv_of_peer.shape[0] // KVH
    if repeat * KVH == kv_of_peer.shape[0] and np.array_equal(kv_of_peer, np.arange(kv_of_peer.shape[0]) // repeat):
        spread = jnp.broadcast_to(split, (tok_rows, KVH, repeat, HD)).reshape(tok_rows, -1, HD)
    else:
        spread = jnp.take(split[:, :, 0], kv_of_peer, axis=1)
    return spread.transpose(1, 0, 2)


def partner_swap(x, pairs):
    return lax.ppermute(x, "row", pairs)


def partial_attention(query_block, query_pos, keys, values, key_pos_cache, key_pos_slab, cache_rows, first_pos):
    cache_ok = jnp.broadcast_to((key_pos_cache < first_pos)[None, :], (query_pos.shape[0], cache_rows))
    slab_ok = key_pos_slab[None, :] <= query_pos[:, None]
    allowed = jnp.concatenate([cache_ok, slab_ok], axis=1)[:, None, :]
    score_scale = 1.0 / math.sqrt(HD)
    scores = jnp.einsum("thd,nd->thn", query_block, keys, preferred_element_type=jnp.float32) * score_scale
    row_max = jnp.max(jnp.where(allowed, scores, -jnp.inf), axis=-1)
    exponent = jnp.where(allowed, jnp.exp(scores - row_max[..., None]), 0.0)
    row_sum = jnp.sum(exponent, axis=-1)
    summed = jnp.einsum(
        "thn,nd->thd", exponent.astype(jnp.bfloat16), values, preferred_element_type=jnp.float32
    )
    return row_max, row_sum, summed


def swap(x, axes, pairs):
    return lax.ppermute(x, axes, pairs)


def decode(codes):
    codes = codes.astype(jnp.float32)
    return codes[..., 0] * code_base + codes[..., 1]


def send_kernel(q_ref, k_ref, v_ref, p_ref, o_ref):
    seq_count = o_ref.shape[0]
    tok_rows = q_ref.shape[0]
    half = tok_rows // 2
    q_width = q_ref.shape[1] // (seq_count // 2)
    q_len = tok_rows * q_width
    lanes = lax.broadcasted_iota(jnp.int32, (1, 128), 1)
    row = jnp.zeros((1, 128), jnp.float32)
    for t in range(tok_rows):
        pos = p_ref[0, t]
        row = jnp.where(lanes == 2 * t, (pos // code_base).astype(jnp.float32), row)
        row = jnp.where(lanes == 2 * t + 1, (pos % code_base).astype(jnp.float32), row)
    row = row.astype(o_ref.dtype)
    for s in range(seq_count):
        group, pair, head = s // 2, s % 2, s // (seq_count // KVH)
        for t in range(tok_rows):
            o_ref[s : s + 1, t * q_width : (t + 1) * q_width] = q_ref[t : t + 1, group * q_width : (group + 1) * q_width]
        for t in range(half):
            k = pair * half + t
            base = q_len + t * 2 * HD
            o_ref[s : s + 1, base : base + HD] = k_ref[k : k + 1, head * HD : (head + 1) * HD]
            o_ref[s : s + 1, base + HD : base + 2 * HD] = v_ref[k : k + 1, head * HD : (head + 1) * HD]
        o_ref[s : s + 1, q_len + half * 2 * HD :] = row


def build_send(queries, new_keys, new_values, positions, seq_count):
    tok_rows = queries.shape[0]
    width = tok_rows * (queries.shape[1] // (seq_count // 2)) + (tok_rows // 2) * 2 * HD + 128
    return pl.pallas_call(
        send_kernel,
        in_specs=[pl.BlockSpec(memory_space=pltpu.VMEM)] * 3 + [pl.BlockSpec(memory_space=pltpu.SMEM)],
        out_specs=pl.BlockSpec(memory_space=pltpu.VMEM),
        out_shape=jax.ShapeDtypeStruct((seq_count, width), queries.dtype),
    )(queries, new_keys, new_values, positions.reshape(1, -1))


def on_device(queries, new_keys, new_values, positions, cache_keys, cache_values, slab_start):
    seq_count = lax.axis_size("seq")
    cell_axes = ("row", "col")
    row_count = lax.axis_size("row")
    col_count = lax.axis_size("col")
    cell_count = row_count * col_count
    heads_dev = HQ // seq_count
    group_size = HQ // KVH
    tok_rows = queries.shape[0]
    first_pos = slab_start[0]
    seq_index = lax.axis_index("seq")
    kv_first = seq_index * heads_dev // group_size
    parity = seq_index % 2
    core = lax.axis_index("row") % 2
    quarter = parity * 2 + core
    core_pairs = [(r, r ^ 1) for r in range(row_count)]
    seq_pairs = [(q, q ^ 1) for q in range(seq_count)]
    diag_pairs = [(q * row_count + r, (q ^ 1) * row_count + (r ^ 1)) for q in range(seq_count) for r in range(row_count)]
    width = 2 * HD
    pair_heads = 2 * heads_dev
    half_tok = tok_rows // 2

    send = build_send(queries, new_keys, new_values, positions, seq_count)
    recv = lax.all_to_all(send, "seq", 0, 0, tiled=True)
    q_len = tok_rows * pair_heads * HD
    kvp_len = half_tok * width
    slab_rows = seq_count * tok_rows
    query_block = recv[:, :q_len].reshape(slab_rows, pair_heads, HD)
    slab_kv = recv[:, q_len : q_len + kvp_len].reshape(seq_count * half_tok, width)
    got_codes = recv[:, q_len + kvp_len : q_len + kvp_len + tok_rows * 2].reshape(seq_count, tok_rows, 2)
    own_pos = decode(got_codes.reshape(slab_rows, 2))
    slab_codes = lax.dynamic_slice_in_dim(got_codes, parity * half_tok, half_tok, 1).reshape(seq_count * half_tok, 2)

    partner_q = swap(
        jnp.concatenate([query_block.reshape(slab_rows, -1), got_codes.reshape(slab_rows, 2)], axis=1), "row", core_pairs
    )
    partner_block = partner_q[:, : pair_heads * HD].reshape(slab_rows, pair_heads, HD)
    partner_pos = decode(partner_q[:, pair_heads * HD :])

    cache_block = jnp.concatenate(
        [
            lax.dynamic_slice_in_dim(cache_keys, kv_first * HD, HD, 1),
            lax.dynamic_slice_in_dim(cache_values, kv_first * HD, HD, 1),
        ],
        axis=1,
    )
    cache_len = cache_block.shape[0]
    part_cache = cache_len // 4
    half_slab = slab_kv.shape[0] // 2
    code_rows = jnp.pad(slab_codes.reshape(2, half_slab * 2), ((0, 0), (0, width - half_slab * 2)))
    cache_pair = lax.dynamic_slice_in_dim(cache_block, parity * 2 * part_cache, 2 * part_cache, 0)
    halves = jnp.stack(
        [
            jnp.concatenate(
                [
                    cache_pair[b * part_cache : (b + 1) * part_cache],
                    slab_kv[b * half_slab : (b + 1) * half_slab],
                    code_rows[b : b + 1],
                ],
                axis=0,
            )
            for b in range(2)
        ]
    )
    per_dest = jnp.broadcast_to(
        halves[None, :, None], (row_count // 2, 2, col_count) + halves.shape[1:]
    ).reshape((cell_count,) + halves.shape[1:])
    every = lax.all_to_all(per_dest, cell_axes, 0, 0, tiled=True)
    cache_got = every[:, :part_cache].reshape(-1, width)
    slab_got = every[:, part_cache : part_cache + half_slab].reshape(-1, width)
    key_pos_slab = decode(every[:, part_cache + half_slab, : 2 * half_slab].reshape(-1, 2))
    key_pos_cache = (
        jnp.arange(cell_count, dtype=jnp.int32)[:, None] * cache_len
        + quarter * part_cache
        + jnp.arange(part_cache, dtype=jnp.int32)[None, :]
    ).reshape(-1)
    keys = jnp.concatenate([cache_got[:, :HD], slab_got[:, :HD]], axis=0)
    values = jnp.concatenate([cache_got[:, HD:], slab_got[:, HD:]], axis=0)

    both_q = jnp.concatenate([query_block, partner_block], axis=0)
    both_pos = jnp.concatenate([own_pos, partner_pos], axis=0)
    row_max, row_sum, summed = partial_attention(
        both_q, both_pos, keys, values, key_pos_cache, key_pos_slab, cache_got.shape[0], first_pos
    )

    theirs = jnp.concatenate(
        [summed[slab_rows:].reshape(slab_rows, -1), row_max[slab_rows:], row_sum[slab_rows:]], axis=1
    )
    got = swap(theirs, "row", core_pairs)
    split_at = pair_heads * HD
    other_summed = got[:, :split_at].reshape(slab_rows, pair_heads, HD)
    other_max = got[:, split_at : split_at + pair_heads]
    other_sum = got[:, split_at + pair_heads :]
    mine_max = row_max[:slab_rows]
    top = jnp.maximum(mine_max, other_max)
    scale_mine = jnp.exp(mine_max - top)
    scale_other = jnp.exp(other_max - top)
    numerator = summed[:slab_rows] * scale_mine[..., None] + other_summed * scale_other[..., None]
    denominator = row_sum[:slab_rows] * scale_mine + other_sum * scale_other
    normed = (numerator / denominator[..., None]).astype(jnp.bfloat16).reshape(slab_rows, -1)
    log_weight = top + jnp.log(denominator)
    pieces = []
    rest = log_weight
    for _ in range(3):
        piece = lax.reduce_precision(rest, exponent_bits=8, mantissa_bits=7)
        pieces.append(piece.astype(jnp.bfloat16))
        rest = rest - piece
    coded = jnp.stack(pieces, axis=1).reshape(slab_rows, -1)
    code_width = 128 * pl_cdiv(coded.shape[1], 128)
    coded = jnp.pad(coded, ((0, 0), (0, code_width - coded.shape[1])))
    partial = jnp.concatenate([normed, coded], axis=1)

    back = lax.all_to_all(partial.reshape(seq_count, tok_rows, -1), "seq", 0, 0, tiled=True)
    back = back.reshape(seq_count // 2, 2, tok_rows, -1)
    half_num = back[..., :split_at].astype(jnp.float32).reshape(seq_count // 2, 2, tok_rows, pair_heads, HD)
    half_log = (
        back[..., split_at : split_at + 3 * pair_heads]
        .astype(jnp.float32)
        .reshape(seq_count // 2, 2, tok_rows, 3, pair_heads)
        .sum(axis=3)
    )
    best = jnp.maximum(half_log[:, 0], half_log[:, 1])
    w0 = jnp.exp(half_log[:, 0] - best)
    w1 = jnp.exp(half_log[:, 1] - best)
    num = half_num[:, 0] * w0[..., None] + half_num[:, 1] * w1[..., None]
    context = (num / (w0 + w1)[..., None]).astype(jnp.bfloat16)
    return context.transpose(1, 0, 2, 3).reshape(tok_rows, -1)


def pl_cdiv(a, b):
    return (a + b - 1) // b


def pl_heads(pair, heads_dev):
    return pair * heads_dev


def solution(mesh):
    in_specs = (
        P(("seq", "row", "col"), None),
        P(("seq", "row", "col"), None),
        P(("seq", "row", "col"), None),
        P(("seq", "row", "col")),
        P(("row", "col"), None),
        P(("row", "col"), None),
        P(),
    )
    out_specs = P(("seq", "row", "col"), None)
    return jax.shard_map(
        on_device, mesh=mesh, in_specs=in_specs, out_specs=out_specs, check_vma=False
    )
```

```python
import math

import numpy as np
import jax
import jax.numpy as jnp
from jax import lax
from jax.sharding import PartitionSpec as P
from jax.experimental import pallas as pl
from jax.experimental.pallas import tpu as pltpu

HQ = 64
KVH = 8
HD = 128

far_position = 1073741824
code_base = 256


def gather_cells(block, cell_axes, cell_count):
    spread = jnp.broadcast_to(block[None], (cell_count,) + block.shape)
    return lax.all_to_all(spread, cell_axes, 0, 0, tiled=True)


def pick_heads(rows, kv_of_peer, tok_rows):
    split = rows.reshape(tok_rows, KVH, 1, HD)
    repeat = kv_of_peer.shape[0] // KVH
    if repeat * KVH == kv_of_peer.shape[0] and np.array_equal(kv_of_peer, np.arange(kv_of_peer.shape[0]) // repeat):
        spread = jnp.broadcast_to(split, (tok_rows, KVH, repeat, HD)).reshape(tok_rows, -1, HD)
    else:
        spread = jnp.take(split[:, :, 0], kv_of_peer, axis=1)
    return spread.transpose(1, 0, 2)


def partner_swap(x, pairs):
    return lax.ppermute(x, "row", pairs)


def partial_attention(query_block, query_pos, keys, values, key_pos_cache, key_pos_slab, cache_rows, first_pos):
    cache_ok = jnp.broadcast_to((key_pos_cache < first_pos)[None, :], (query_pos.shape[0], cache_rows))
    slab_ok = key_pos_slab[None, :] <= query_pos[:, None]
    allowed = jnp.concatenate([cache_ok, slab_ok], axis=1)[:, None, :]
    score_scale = 1.0 / math.sqrt(HD)
    scores = jnp.einsum("thd,nd->thn", query_block, keys, preferred_element_type=jnp.float32) * score_scale
    row_max = jnp.max(jnp.where(allowed, scores, -jnp.inf), axis=-1)
    exponent = jnp.where(allowed, jnp.exp(scores - row_max[..., None]), 0.0)
    row_sum = jnp.sum(exponent, axis=-1)
    summed = jnp.einsum(
        "thn,nd->thd", exponent.astype(jnp.bfloat16), values, preferred_element_type=jnp.float32
    )
    return row_max, row_sum, summed


def swap(x, axes, pairs):
    return lax.ppermute(x, axes, pairs)


def decode(codes):
    codes = codes.astype(jnp.float32)
    return codes[..., 0] * code_base + codes[..., 1]


def send_kernel(q_ref, k_ref, v_ref, p_ref, o_ref):
    seq_count = o_ref.shape[0]
    tok_rows = q_ref.shape[0]
    half = tok_rows // 2
    q_width = q_ref.shape[1] // (seq_count // 2)
    lanes = lax.broadcasted_iota(jnp.int32, (1, 128), 1)
    row = jnp.zeros((1, 128), jnp.float32)
    for t in range(tok_rows):
        pos = p_ref[0, t]
        row = jnp.where(lanes == 2 * t, (pos // code_base).astype(jnp.float32), row)
        row = jnp.where(lanes == 2 * t + 1, (pos % code_base).astype(jnp.float32), row)
    row = row.astype(o_ref.dtype)
    zeros = jnp.zeros((1, 128), o_ref.dtype)
    for s in range(seq_count):
        group, pair, head = s // 2, s % 2, s // (seq_count // KVH)
        for h in range(2):
            for j in range(half):
                t = h * half + j
                o_ref[s, h : h + 1, j * q_width : (j + 1) * q_width] = q_ref[t : t + 1, group * q_width : (group + 1) * q_width]
            k = pair * half + h
            base = half * q_width
            o_ref[s, h : h + 1, base : base + HD] = k_ref[k : k + 1, head * HD : (head + 1) * HD]
            o_ref[s, h : h + 1, base + HD : base + 2 * HD] = v_ref[k : k + 1, head * HD : (head + 1) * HD]
            o_ref[s, h : h + 1, base + 2 * HD :] = row if h == 0 else zeros


def build_send(queries, new_keys, new_values, positions, seq_count):
    tok_rows = queries.shape[0]
    width = (tok_rows // 2) * (queries.shape[1] // (seq_count // 2)) + 2 * HD + 128
    return pl.pallas_call(
        send_kernel,
        in_specs=[pl.BlockSpec(memory_space=pltpu.VMEM)] * 3 + [pl.BlockSpec(memory_space=pltpu.SMEM)],
        out_specs=pl.BlockSpec(memory_space=pltpu.VMEM),
        out_shape=jax.ShapeDtypeStruct((seq_count, 2, width), queries.dtype),
    )(queries, new_keys, new_values, positions.reshape(1, -1))


def on_device(queries, new_keys, new_values, positions, cache_keys, cache_values, slab_start):
    seq_count = lax.axis_size("seq")
    cell_axes = ("row", "col")
    row_count = lax.axis_size("row")
    col_count = lax.axis_size("col")
    cell_count = row_count * col_count
    heads_dev = HQ // seq_count
    group_size = HQ // KVH
    tok_rows = queries.shape[0]
    first_pos = slab_start[0]
    seq_index = lax.axis_index("seq")
    kv_first = seq_index * heads_dev // group_size
    parity = seq_index % 2
    core = lax.axis_index("row") % 2
    quarter = parity * 2 + core
    core_pairs = [(r, r ^ 1) for r in range(row_count)]
    seq_pairs = [(q, q ^ 1) for q in range(seq_count)]
    diag_pairs = [(q * row_count + r, (q ^ 1) * row_count + (r ^ 1)) for q in range(seq_count) for r in range(row_count)]
    width = 2 * HD
    pair_heads = 2 * heads_dev
    half_tok = tok_rows // 2

    send = build_send(queries, new_keys, new_values, positions, seq_count)
    recv = lax.all_to_all(send, "seq", 0, 0, tiled=True)
    q_half = half_tok * pair_heads * HD
    slab_rows = seq_count * tok_rows
    query_block = recv[:, :, :q_half].reshape(slab_rows, pair_heads, HD)
    slab_kv = recv[:, :, q_half : q_half + width].reshape(seq_count * half_tok, width)
    got_codes = recv[:, 0, q_half + width : q_half + width + tok_rows * 2].reshape(seq_count, tok_rows, 2)
    own_pos = decode(got_codes.reshape(slab_rows, 2))
    slab_codes = lax.dynamic_slice_in_dim(got_codes, parity * half_tok, half_tok, 1).reshape(seq_count * half_tok, 2)

    partner_q = swap(
        jnp.concatenate([query_block.reshape(slab_rows, -1), got_codes.reshape(slab_rows, 2)], axis=1), "row", core_pairs
    )
    partner_block = partner_q[:, : pair_heads * HD].reshape(slab_rows, pair_heads, HD)
    partner_pos = decode(partner_q[:, pair_heads * HD :])

    cache_block = jnp.concatenate(
        [
            lax.dynamic_slice_in_dim(cache_keys, kv_first * HD, HD, 1),
            lax.dynamic_slice_in_dim(cache_values, kv_first * HD, HD, 1),
        ],
        axis=1,
    )
    cache_len = cache_block.shape[0]
    part_cache = cache_len // 4
    half_slab = slab_kv.shape[0] // 2
    code_rows = jnp.pad(slab_codes.reshape(2, half_slab * 2), ((0, 0), (0, width - half_slab * 2)))
    cache_pair = lax.dynamic_slice_in_dim(cache_block, parity * 2 * part_cache, 2 * part_cache, 0)
    halves = jnp.stack(
        [
            jnp.concatenate(
                [
                    cache_pair[b * part_cache : (b + 1) * part_cache],
                    slab_kv[b * half_slab : (b + 1) * half_slab],
                    code_rows[b : b + 1],
                ],
                axis=0,
            )
            for b in range(2)
        ]
    )
    per_dest = jnp.broadcast_to(
        halves[None, :, None], (row_count // 2, 2, col_count) + halves.shape[1:]
    ).reshape((cell_count,) + halves.shape[1:])
    every = lax.all_to_all(per_dest, cell_axes, 0, 0, tiled=True)
    cache_got = every[:, :part_cache].reshape(-1, width)
    slab_got = every[:, part_cache : part_cache + half_slab].reshape(-1, width)
    key_pos_slab = decode(every[:, part_cache + half_slab, : 2 * half_slab].reshape(-1, 2))
    key_pos_cache = (
        jnp.arange(cell_count, dtype=jnp.int32)[:, None] * cache_len
        + quarter * part_cache
        + jnp.arange(part_cache, dtype=jnp.int32)[None, :]
    ).reshape(-1)
    keys = jnp.concatenate([cache_got[:, :HD], slab_got[:, :HD]], axis=0)
    values = jnp.concatenate([cache_got[:, HD:], slab_got[:, HD:]], axis=0)

    both_q = jnp.concatenate([query_block, partner_block], axis=0)
    both_pos = jnp.concatenate([own_pos, partner_pos], axis=0)
    row_max, row_sum, summed = partial_attention(
        both_q, both_pos, keys, values, key_pos_cache, key_pos_slab, cache_got.shape[0], first_pos
    )

    theirs = jnp.concatenate(
        [summed[slab_rows:].reshape(slab_rows, -1), row_max[slab_rows:], row_sum[slab_rows:]], axis=1
    )
    got = swap(theirs, "row", core_pairs)
    split_at = pair_heads * HD
    other_summed = got[:, :split_at].reshape(slab_rows, pair_heads, HD)
    other_max = got[:, split_at : split_at + pair_heads]
    other_sum = got[:, split_at + pair_heads :]
    mine_max = row_max[:slab_rows]
    top = jnp.maximum(mine_max, other_max)
    scale_mine = jnp.exp(mine_max - top)
    scale_other = jnp.exp(other_max - top)
    numerator = summed[:slab_rows] * scale_mine[..., None] + other_summed * scale_other[..., None]
    denominator = row_sum[:slab_rows] * scale_mine + other_sum * scale_other
    normed = (numerator / denominator[..., None]).astype(jnp.bfloat16).reshape(slab_rows, -1)
    log_weight = top + jnp.log(denominator)
    pieces = []
    rest = log_weight
    for _ in range(3):
        piece = lax.reduce_precision(rest, exponent_bits=8, mantissa_bits=7)
        pieces.append(piece.astype(jnp.bfloat16))
        rest = rest - piece
    coded = jnp.stack(pieces, axis=1).reshape(slab_rows, -1)
    code_width = 128 * pl_cdiv(coded.shape[1], 128)
    coded = jnp.pad(coded, ((0, 0), (0, code_width - coded.shape[1])))
    partial = jnp.concatenate([normed, coded], axis=1)

    back = lax.all_to_all(partial.reshape(seq_count, tok_rows, -1), "seq", 0, 0, tiled=True)
    back = back.reshape(seq_count // 2, 2, tok_rows, -1)
    half_num = back[..., :split_at].astype(jnp.float32).reshape(seq_count // 2, 2, tok_rows, pair_heads, HD)
    half_log = (
        back[..., split_at : split_at + 3 * pair_heads]
        .astype(jnp.float32)
        .reshape(seq_count // 2, 2, tok_rows, 3, pair_heads)
        .sum(axis=3)
    )
    best = jnp.maximum(half_log[:, 0], half_log[:, 1])
    w0 = jnp.exp(half_log[:, 0] - best)
    w1 = jnp.exp(half_log[:, 1] - best)
    num = half_num[:, 0] * w0[..., None] + half_num[:, 1] * w1[..., None]
    context = (num / (w0 + w1)[..., None]).astype(jnp.bfloat16)
    return context.transpose(1, 0, 2, 3).reshape(tok_rows, -1)


def pl_cdiv(a, b):
    return (a + b - 1) // b


def pl_heads(pair, heads_dev):
    return pair * heads_dev


def solution(mesh):
    in_specs = (
        P(("seq", "row", "col"), None),
        P(("seq", "row", "col"), None),
        P(("seq", "row", "col"), None),
        P(("seq", "row", "col")),
        P(("row", "col"), None),
        P(("row", "col"), None),
        P(),
    )
    out_specs = P(("seq", "row", "col"), None)
    return jax.shard_map(
        on_device, mesh=mesh, in_specs=in_specs, out_specs=out_specs, check_vma=False
    )
```

```python
import math

import numpy as np
import jax
import jax.numpy as jnp
from jax import lax
from jax.sharding import PartitionSpec as P
from jax.experimental import pallas as pl
from jax.experimental.pallas import tpu as pltpu

HQ = 64
KVH = 8
HD = 128

far_position = 1073741824
code_base = 256


def gather_cells(block, cell_axes, cell_count):
    spread = jnp.broadcast_to(block[None], (cell_count,) + block.shape)
    return lax.all_to_all(spread, cell_axes, 0, 0, tiled=True)


def pick_heads(rows, kv_of_peer, tok_rows):
    split = rows.reshape(tok_rows, KVH, 1, HD)
    repeat = kv_of_peer.shape[0] // KVH
    if repeat * KVH == kv_of_peer.shape[0] and np.array_equal(kv_of_peer, np.arange(kv_of_peer.shape[0]) // repeat):
        spread = jnp.broadcast_to(split, (tok_rows, KVH, repeat, HD)).reshape(tok_rows, -1, HD)
    else:
        spread = jnp.take(split[:, :, 0], kv_of_peer, axis=1)
    return spread.transpose(1, 0, 2)


def partner_swap(x, pairs):
    return lax.ppermute(x, "row", pairs)


def partial_attention(query_block, query_pos, keys, values, key_pos_cache, key_pos_slab, cache_rows, first_pos):
    cache_ok = jnp.broadcast_to((key_pos_cache < first_pos)[None, :], (query_pos.shape[0], cache_rows))
    slab_ok = key_pos_slab[None, :] <= query_pos[:, None]
    allowed = jnp.concatenate([cache_ok, slab_ok], axis=1)[:, None, :]
    score_scale = 1.0 / math.sqrt(HD)
    scores = jnp.einsum("thd,nd->thn", query_block, keys, preferred_element_type=jnp.float32) * score_scale
    row_max = jnp.max(jnp.where(allowed, scores, -jnp.inf), axis=-1)
    exponent = jnp.where(allowed, jnp.exp(scores - row_max[..., None]), 0.0)
    row_sum = jnp.sum(exponent, axis=-1)
    summed = jnp.einsum(
        "thn,nd->thd", exponent.astype(jnp.bfloat16), values, preferred_element_type=jnp.float32
    )
    return row_max, row_sum, summed


def swap(x, axes, pairs):
    return lax.ppermute(x, axes, pairs)


def decode(codes):
    codes = codes.astype(jnp.float32)
    return codes[..., 0] * code_base + codes[..., 1]


def send_kernel(q_ref, k_ref, v_ref, p_ref, o_ref):
    seq_count = o_ref.shape[0]
    tok_rows = q_ref.shape[0]
    half = tok_rows // 2
    q_width = q_ref.shape[1] // (seq_count // 2)
    lanes = lax.broadcasted_iota(jnp.int32, (1, 128), 1)
    row = jnp.zeros((1, 128), jnp.float32)
    for t in range(tok_rows):
        pos = p_ref[0, t]
        row = jnp.where(lanes == 2 * t, (pos // code_base).astype(jnp.float32), row)
        row = jnp.where(lanes == 2 * t + 1, (pos % code_base).astype(jnp.float32), row)
    row = row.astype(o_ref.dtype)
    zeros = jnp.zeros((1, 128), o_ref.dtype)
    for s in range(seq_count):
        group, pair, head = s // 2, s % 2, s // (seq_count // KVH)
        for h in range(2):
            for j in range(half):
                t = h * half + j
                o_ref[s, h : h + 1, j * q_width : (j + 1) * q_width] = q_ref[t : t + 1, group * q_width : (group + 1) * q_width]
            k = pair * half + h
            base = half * q_width
            o_ref[s, h : h + 1, base : base + HD] = k_ref[k : k + 1, head * HD : (head + 1) * HD]
            o_ref[s, h : h + 1, base + HD : base + 2 * HD] = v_ref[k : k + 1, head * HD : (head + 1) * HD]
            o_ref[s, h : h + 1, base + 2 * HD :] = row if h == 0 else zeros


def build_send(queries, new_keys, new_values, positions, seq_count):
    tok_rows = queries.shape[0]
    width = (tok_rows // 2) * (queries.shape[1] // (seq_count // 2)) + 2 * HD + 128
    return pl.pallas_call(
        send_kernel,
        in_specs=[pl.BlockSpec(memory_space=pltpu.VMEM)] * 3 + [pl.BlockSpec(memory_space=pltpu.SMEM)],
        out_specs=pl.BlockSpec(memory_space=pltpu.VMEM),
        out_shape=jax.ShapeDtypeStruct((seq_count, 2, width), queries.dtype),
    )(queries, new_keys, new_values, positions.reshape(1, -1))


def on_device(queries, new_keys, new_values, positions, cache_keys, cache_values, slab_start):
    seq_count = lax.axis_size("seq")
    cell_axes = ("row", "col")
    row_count = lax.axis_size("row")
    col_count = lax.axis_size("col")
    cell_count = row_count * col_count
    heads_dev = HQ // seq_count
    group_size = HQ // KVH
    tok_rows = queries.shape[0]
    first_pos = slab_start[0]
    seq_index = lax.axis_index("seq")
    kv_first = seq_index * heads_dev // group_size
    parity = seq_index % 2
    core = lax.axis_index("row") % 2
    quarter = parity * 2 + core
    core_pairs = [(r, r ^ 1) for r in range(row_count)]
    seq_pairs = [(q, q ^ 1) for q in range(seq_count)]
    diag_pairs = [(q * row_count + r, (q ^ 1) * row_count + (r ^ 1)) for q in range(seq_count) for r in range(row_count)]
    width = 2 * HD
    pair_heads = 2 * heads_dev
    half_tok = tok_rows // 2

    send = build_send(queries, new_keys, new_values, positions, seq_count)
    recv = lax.all_to_all(send, "seq", 0, 0, tiled=True)
    q_half = half_tok * pair_heads * HD
    slab_rows = seq_count * tok_rows
    query_block = recv[:, :, :q_half].reshape(slab_rows, pair_heads, HD)
    slab_kv = recv[:, :, q_half : q_half + width].reshape(seq_count * half_tok, width)
    got_codes = recv[:, 0, q_half + width : q_half + width + tok_rows * 2].reshape(seq_count, tok_rows, 2)
    own_pos = decode(got_codes.reshape(slab_rows, 2))
    slab_codes = lax.dynamic_slice_in_dim(got_codes, parity * half_tok, half_tok, 1).reshape(seq_count * half_tok, 2)

    partner_q = swap(
        jnp.concatenate([query_block.reshape(slab_rows, -1), got_codes.reshape(slab_rows, 2)], axis=1), "row", core_pairs
    )
    partner_block = partner_q[:, : pair_heads * HD].reshape(slab_rows, pair_heads, HD)
    partner_pos = decode(partner_q[:, pair_heads * HD :])

    cache_block = jnp.concatenate(
        [
            lax.dynamic_slice_in_dim(cache_keys, kv_first * HD, HD, 1),
            lax.dynamic_slice_in_dim(cache_values, kv_first * HD, HD, 1),
        ],
        axis=1,
    )
    cache_len = cache_block.shape[0]
    part_cache = cache_len // 4
    half_slab = slab_kv.shape[0] // 2
    code_rows = jnp.pad(slab_codes.reshape(2, half_slab * 2), ((0, 0), (0, width - half_slab * 2)))
    cache_pair = lax.dynamic_slice_in_dim(cache_block, parity * 2 * part_cache, 2 * part_cache, 0)
    halves = jnp.stack(
        [
            jnp.concatenate(
                [
                    cache_pair[b * part_cache : (b + 1) * part_cache],
                    slab_kv[b * half_slab : (b + 1) * half_slab],
                    code_rows[b : b + 1],
                ],
                axis=0,
            )
            for b in range(2)
        ]
    )
    per_dest = jnp.broadcast_to(
        halves[None, :, None], (row_count // 2, 2, col_count) + halves.shape[1:]
    ).reshape((cell_count,) + halves.shape[1:])
    every = lax.all_to_all(per_dest, cell_axes, 0, 0, tiled=True)
    cache_got = every[:, :part_cache].reshape(-1, width)
    slab_got = every[:, part_cache : part_cache + half_slab].reshape(-1, width)
    key_pos_slab = decode(every[:, part_cache + half_slab, : 2 * half_slab].reshape(-1, 2))
    key_pos_cache = (
        jnp.arange(cell_count, dtype=jnp.int32)[:, None] * cache_len
        + quarter * part_cache
        + jnp.arange(part_cache, dtype=jnp.int32)[None, :]
    ).reshape(-1)
    keys = jnp.concatenate([cache_got[:, :HD], slab_got[:, :HD]], axis=0)
    values = jnp.concatenate([cache_got[:, HD:], slab_got[:, HD:]], axis=0)

    cache_count = cache_got.shape[0]
    their_max, their_sum, their_summed = partial_attention(
        partner_block, partner_pos, keys, values, key_pos_cache, key_pos_slab, cache_count, first_pos
    )
    theirs = jnp.concatenate([their_summed.reshape(slab_rows, -1), their_max, their_sum], axis=1)
    got = swap(theirs, "row", core_pairs)
    mine_max, mine_sum, mine_summed = partial_attention(
        query_block, own_pos, keys, values, key_pos_cache, key_pos_slab, cache_count, first_pos
    )

    split_at = pair_heads * HD
    other_summed = got[:, :split_at].reshape(slab_rows, pair_heads, HD)
    other_max = got[:, split_at : split_at + pair_heads]
    other_sum = got[:, split_at + pair_heads :]
    top = jnp.maximum(mine_max, other_max)
    scale_mine = jnp.exp(mine_max - top)
    scale_other = jnp.exp(other_max - top)
    numerator = mine_summed * scale_mine[..., None] + other_summed * scale_other[..., None]
    denominator = mine_sum * scale_mine + other_sum * scale_other
    normed = (numerator / denominator[..., None]).astype(jnp.bfloat16).reshape(slab_rows, -1)
    log_weight = top + jnp.log(denominator)
    pieces = []
    rest = log_weight
    for _ in range(3):
        piece = lax.reduce_precision(rest, exponent_bits=8, mantissa_bits=7)
        pieces.append(piece.astype(jnp.bfloat16))
        rest = rest - piece
    coded = jnp.stack(pieces, axis=1).reshape(slab_rows, -1)
    code_width = 128 * pl_cdiv(coded.shape[1], 128)
    coded = jnp.pad(coded, ((0, 0), (0, code_width - coded.shape[1])))
    partial = jnp.concatenate([normed, coded], axis=1)

    back = lax.all_to_all(partial.reshape(seq_count, tok_rows, -1), "seq", 0, 0, tiled=True)
    back = back.reshape(seq_count // 2, 2, tok_rows, -1)
    half_num = back[..., :split_at].astype(jnp.float32).reshape(seq_count // 2, 2, tok_rows, pair_heads, HD)
    half_log = (
        back[..., split_at : split_at + 3 * pair_heads]
        .astype(jnp.float32)
        .reshape(seq_count // 2, 2, tok_rows, 3, pair_heads)
        .sum(axis=3)
    )
    best = jnp.maximum(half_log[:, 0], half_log[:, 1])
    w0 = jnp.exp(half_log[:, 0] - best)
    w1 = jnp.exp(half_log[:, 1] - best)
    num = half_num[:, 0] * w0[..., None] + half_num[:, 1] * w1[..., None]
    context = (num / (w0 + w1)[..., None]).astype(jnp.bfloat16)
    return context.transpose(1, 0, 2, 3).reshape(tok_rows, -1)


def pl_cdiv(a, b):
    return (a + b - 1) // b


def pl_heads(pair, heads_dev):
    return pair * heads_dev


def solution(mesh):
    in_specs = (
        P(("seq", "row", "col"), None),
        P(("seq", "row", "col"), None),
        P(("seq", "row", "col"), None),
        P(("seq", "row", "col")),
        P(("row", "col"), None),
        P(("row", "col"), None),
        P(),
    )
    out_specs = P(("seq", "row", "col"), None)
    return jax.shard_map(
        on_device, mesh=mesh, in_specs=in_specs, out_specs=out_specs, check_vma=False
    )
```

```python
import math

import numpy as np
import jax
import jax.numpy as jnp
from jax import lax
from jax.sharding import PartitionSpec as P
from jax.experimental import pallas as pl
from jax.experimental.pallas import tpu as pltpu

HQ = 64
KVH = 8
HD = 128

far_position = 1073741824
code_base = 256


def gather_cells(block, cell_axes, cell_count):
    spread = jnp.broadcast_to(block[None], (cell_count,) + block.shape)
    return lax.all_to_all(spread, cell_axes, 0, 0, tiled=True)


def pick_heads(rows, kv_of_peer, tok_rows):
    split = rows.reshape(tok_rows, KVH, 1, HD)
    repeat = kv_of_peer.shape[0] // KVH
    if repeat * KVH == kv_of_peer.shape[0] and np.array_equal(kv_of_peer, np.arange(kv_of_peer.shape[0]) // repeat):
        spread = jnp.broadcast_to(split, (tok_rows, KVH, repeat, HD)).reshape(tok_rows, -1, HD)
    else:
        spread = jnp.take(split[:, :, 0], kv_of_peer, axis=1)
    return spread.transpose(1, 0, 2)


def partner_swap(x, pairs):
    return lax.ppermute(x, "row", pairs)


def partial_attention(query_block, query_pos, keys, values, key_pos_cache, key_pos_slab, cache_rows, first_pos):
    cache_ok = jnp.broadcast_to((key_pos_cache < first_pos)[None, :], (query_pos.shape[0], cache_rows))
    slab_ok = key_pos_slab[None, :] <= query_pos[:, None]
    allowed = jnp.concatenate([cache_ok, slab_ok], axis=1)[:, None, :]
    score_scale = 1.0 / math.sqrt(HD)
    scores = jnp.einsum("thd,nd->thn", query_block, keys, preferred_element_type=jnp.float32) * score_scale
    row_max = jnp.max(jnp.where(allowed, scores, -jnp.inf), axis=-1)
    exponent = jnp.where(allowed, jnp.exp(scores - row_max[..., None]), 0.0)
    row_sum = jnp.sum(exponent, axis=-1)
    summed = jnp.einsum(
        "thn,nd->thd", exponent.astype(jnp.bfloat16), values, preferred_element_type=jnp.float32
    )
    return row_max, row_sum, summed


def swap(x, axes, pairs):
    return lax.ppermute(x, axes, pairs)


def decode(codes):
    codes = codes.astype(jnp.float32)
    return codes[..., 0] * code_base + codes[..., 1]


def send_kernel(q_ref, k_ref, v_ref, p_ref, o_ref):
    seq_count = o_ref.shape[0]
    tok_rows = q_ref.shape[0]
    half = tok_rows // 2
    q_width = q_ref.shape[1] // (seq_count // 2)
    lanes = lax.broadcasted_iota(jnp.int32, (1, 128), 1)
    row = jnp.zeros((1, 128), jnp.float32)
    for t in range(tok_rows):
        pos = p_ref[0, t]
        row = jnp.where(lanes == 2 * t, (pos // code_base).astype(jnp.float32), row)
        row = jnp.where(lanes == 2 * t + 1, (pos % code_base).astype(jnp.float32), row)
    row = row.astype(o_ref.dtype)
    zeros = jnp.zeros((1, 128), o_ref.dtype)
    for s in range(seq_count):
        group, pair, head = s // 2, s % 2, s // (seq_count // KVH)
        for h in range(2):
            for j in range(half):
                t = h * half + j
                o_ref[s, h : h + 1, j * q_width : (j + 1) * q_width] = q_ref[t : t + 1, group * q_width : (group + 1) * q_width]
            k = pair * half + h
            base = half * q_width
            o_ref[s, h : h + 1, base : base + HD] = k_ref[k : k + 1, head * HD : (head + 1) * HD]
            o_ref[s, h : h + 1, base + HD : base + 2 * HD] = v_ref[k : k + 1, head * HD : (head + 1) * HD]
            o_ref[s, h : h + 1, base + 2 * HD :] = row if h == 0 else zeros


def build_send(queries, new_keys, new_values, positions, seq_count):
    tok_rows = queries.shape[0]
    width = (tok_rows // 2) * (queries.shape[1] // (seq_count // 2)) + 2 * HD + 128
    return pl.pallas_call(
        send_kernel,
        in_specs=[pl.BlockSpec(memory_space=pltpu.VMEM)] * 3 + [pl.BlockSpec(memory_space=pltpu.SMEM)],
        out_specs=pl.BlockSpec(memory_space=pltpu.VMEM),
        out_shape=jax.ShapeDtypeStruct((seq_count, 2, width), queries.dtype),
    )(queries, new_keys, new_values, positions.reshape(1, -1))


def on_device(queries, new_keys, new_values, positions, cache_keys, cache_values, slab_start):
    seq_count = lax.axis_size("seq")
    cell_axes = ("row", "col")
    row_count = lax.axis_size("row")
    col_count = lax.axis_size("col")
    cell_count = row_count * col_count
    heads_dev = HQ // seq_count
    group_size = HQ // KVH
    tok_rows = queries.shape[0]
    first_pos = slab_start[0]
    seq_index = lax.axis_index("seq")
    kv_first = seq_index * heads_dev // group_size
    parity = seq_index % 2
    core = lax.axis_index("row") % 2
    quarter = parity * 2 + core
    core_pairs = [(r, r ^ 1) for r in range(row_count)]
    seq_pairs = [(q, q ^ 1) for q in range(seq_count)]
    diag_pairs = [(q * row_count + r, (q ^ 1) * row_count + (r ^ 1)) for q in range(seq_count) for r in range(row_count)]
    width = 2 * HD
    pair_heads = 2 * heads_dev
    half_tok = tok_rows // 2

    send = build_send(queries, new_keys, new_values, positions, seq_count)
    recv = lax.all_to_all(send, "seq", 0, 0, tiled=True)
    q_half = half_tok * pair_heads * HD
    slab_rows = seq_count * tok_rows
    query_block = recv[:, :, :q_half].reshape(slab_rows, pair_heads, HD)
    slab_kv = recv[:, :, q_half : q_half + width].reshape(seq_count * half_tok, width)
    got_codes = recv[:, 0, q_half + width : q_half + width + tok_rows * 2].reshape(seq_count, tok_rows, 2)
    own_pos = decode(got_codes.reshape(slab_rows, 2))
    slab_codes = lax.dynamic_slice_in_dim(got_codes, parity * half_tok, half_tok, 1).reshape(seq_count * half_tok, 2)

    partner_q = swap(
        jnp.concatenate([query_block.reshape(slab_rows, -1), got_codes.reshape(slab_rows, 2)], axis=1), "row", core_pairs
    )
    partner_block = partner_q[:, : pair_heads * HD].reshape(slab_rows, pair_heads, HD)
    partner_pos = decode(partner_q[:, pair_heads * HD :])

    cache_block = jnp.concatenate(
        [
            lax.dynamic_slice_in_dim(cache_keys, kv_first * HD, HD, 1),
            lax.dynamic_slice_in_dim(cache_values, kv_first * HD, HD, 1),
        ],
        axis=1,
    )
    cache_len = cache_block.shape[0]
    part_cache = cache_len // 4
    half_slab = slab_kv.shape[0] // 2
    code_rows = jnp.pad(slab_codes.reshape(2, half_slab * 2), ((0, 0), (0, width - half_slab * 2)))
    cache_pair = lax.dynamic_slice_in_dim(cache_block, parity * 2 * part_cache, 2 * part_cache, 0)
    halves = jnp.stack(
        [
            jnp.concatenate(
                [
                    cache_pair[b * part_cache : (b + 1) * part_cache],
                    slab_kv[b * half_slab : (b + 1) * half_slab],
                    code_rows[b : b + 1],
                ],
                axis=0,
            )
            for b in range(2)
        ]
    )
    chunk_rows = halves.shape[1] * width // 128
    halves = halves.reshape(2, chunk_rows, 128)
    per_dest = jnp.broadcast_to(
        halves[None, :, None], (row_count // 2, 2, col_count) + halves.shape[1:]
    ).reshape((cell_count,) + halves.shape[1:])
    every = lax.all_to_all(per_dest, cell_axes, 0, 0, tiled=True)
    every = every.reshape(cell_count, -1, width)
    cache_got = every[:, :part_cache].reshape(-1, width)
    slab_got = every[:, part_cache : part_cache + half_slab].reshape(-1, width)
    key_pos_slab = decode(every[:, part_cache + half_slab, : 2 * half_slab].reshape(-1, 2))
    key_pos_cache = (
        jnp.arange(cell_count, dtype=jnp.int32)[:, None] * cache_len
        + quarter * part_cache
        + jnp.arange(part_cache, dtype=jnp.int32)[None, :]
    ).reshape(-1)
    keys = jnp.concatenate([cache_got[:, :HD], slab_got[:, :HD]], axis=0)
    values = jnp.concatenate([cache_got[:, HD:], slab_got[:, HD:]], axis=0)

    cache_count = cache_got.shape[0]
    their_max, their_sum, their_summed = partial_attention(
        partner_block, partner_pos, keys, values, key_pos_cache, key_pos_slab, cache_count, first_pos
    )
    theirs = jnp.concatenate([their_summed.reshape(slab_rows, -1), their_max, their_sum], axis=1)
    got = swap(theirs, "row", core_pairs)
    mine_max, mine_sum, mine_summed = partial_attention(
        query_block, own_pos, keys, values, key_pos_cache, key_pos_slab, cache_count, first_pos
    )

    split_at = pair_heads * HD
    other_summed = got[:, :split_at].reshape(slab_rows, pair_heads, HD)
    other_max = got[:, split_at : split_at + pair_heads]
    other_sum = got[:, split_at + pair_heads :]
    top = jnp.maximum(mine_max, other_max)
    scale_mine = jnp.exp(mine_max - top)
    scale_other = jnp.exp(other_max - top)
    numerator = mine_summed * scale_mine[..., None] + other_summed * scale_other[..., None]
    denominator = mine_sum * scale_mine + other_sum * scale_other
    normed = (numerator / denominator[..., None]).astype(jnp.bfloat16).reshape(slab_rows, -1)
    log_weight = top + jnp.log(denominator)
    pieces = []
    rest = log_weight
    for _ in range(3):
        piece = lax.reduce_precision(rest, exponent_bits=8, mantissa_bits=7)
        pieces.append(piece.astype(jnp.bfloat16))
        rest = rest - piece
    coded = jnp.stack(pieces, axis=1).reshape(slab_rows, -1)
    code_width = 128 * pl_cdiv(coded.shape[1], 128)
    coded = jnp.pad(coded, ((0, 0), (0, code_width - coded.shape[1])))
    partial = jnp.concatenate([normed, coded], axis=1)

    back = lax.all_to_all(partial.reshape(seq_count, tok_rows, -1), "seq", 0, 0, tiled=True)
    back = back.reshape(seq_count // 2, 2, tok_rows, -1)
    half_num = back[..., :split_at].astype(jnp.float32).reshape(seq_count // 2, 2, tok_rows, pair_heads, HD)
    half_log = (
        back[..., split_at : split_at + 3 * pair_heads]
        .astype(jnp.float32)
        .reshape(seq_count // 2, 2, tok_rows, 3, pair_heads)
        .sum(axis=3)
    )
    best = jnp.maximum(half_log[:, 0], half_log[:, 1])
    w0 = jnp.exp(half_log[:, 0] - best)
    w1 = jnp.exp(half_log[:, 1] - best)
    num = half_num[:, 0] * w0[..., None] + half_num[:, 1] * w1[..., None]
    context = (num / (w0 + w1)[..., None]).astype(jnp.bfloat16)
    return context.transpose(1, 0, 2, 3).reshape(tok_rows, -1)


def pl_cdiv(a, b):
    return (a + b - 1) // b


def pl_heads(pair, heads_dev):
    return pair * heads_dev


def solution(mesh):
    in_specs = (
        P(("seq", "row", "col"), None),
        P(("seq", "row", "col"), None),
        P(("seq", "row", "col"), None),
        P(("seq", "row", "col")),
        P(("row", "col"), None),
        P(("row", "col"), None),
        P(),
    )
    out_specs = P(("seq", "row", "col"), None)
    return jax.shard_map(
        on_device, mesh=mesh, in_specs=in_specs, out_specs=out_specs, check_vma=False
    )
```

```python
import math

import numpy as np
import jax
import jax.numpy as jnp
from jax import lax
from jax.sharding import PartitionSpec as P
from jax.experimental import pallas as pl
from jax.experimental.pallas import tpu as pltpu

HQ = 64
KVH = 8
HD = 128

far_position = 1073741824
code_base = 256


def gather_cells(block, cell_axes, cell_count):
    spread = jnp.broadcast_to(block[None], (cell_count,) + block.shape)
    return lax.all_to_all(spread, cell_axes, 0, 0, tiled=True)


def pick_heads(rows, kv_of_peer, tok_rows):
    split = rows.reshape(tok_rows, KVH, 1, HD)
    repeat = kv_of_peer.shape[0] // KVH
    if repeat * KVH == kv_of_peer.shape[0] and np.array_equal(kv_of_peer, np.arange(kv_of_peer.shape[0]) // repeat):
        spread = jnp.broadcast_to(split, (tok_rows, KVH, repeat, HD)).reshape(tok_rows, -1, HD)
    else:
        spread = jnp.take(split[:, :, 0], kv_of_peer, axis=1)
    return spread.transpose(1, 0, 2)


def partner_swap(x, pairs):
    return lax.ppermute(x, "row", pairs)


def partial_attention(query_block, query_pos, keys, values, key_pos_cache, key_pos_slab, cache_rows, first_pos):
    cache_ok = jnp.broadcast_to((key_pos_cache < first_pos)[None, :], (query_pos.shape[0], cache_rows))
    slab_ok = key_pos_slab[None, :] <= query_pos[:, None]
    allowed = jnp.concatenate([cache_ok, slab_ok], axis=1)[:, None, :]
    score_scale = 1.0 / math.sqrt(HD)
    scores = jnp.einsum("thd,nd->thn", query_block, keys, preferred_element_type=jnp.float32) * score_scale
    row_max = jnp.max(jnp.where(allowed, scores, -jnp.inf), axis=-1)
    exponent = jnp.where(allowed, jnp.exp(scores - row_max[..., None]), 0.0)
    row_sum = jnp.sum(exponent, axis=-1)
    summed = jnp.einsum(
        "thn,nd->thd", exponent.astype(jnp.bfloat16), values, preferred_element_type=jnp.float32
    )
    return row_max, row_sum, summed


def swap(x, axes, pairs):
    return lax.ppermute(x, axes, pairs)


def decode(codes):
    codes = codes.astype(jnp.float32)
    return codes[..., 0] * code_base + codes[..., 1]


def send_kernel(q_ref, k_ref, v_ref, p_ref, o_ref):
    seq_count = o_ref.shape[0]
    tok_rows = q_ref.shape[0]
    half = tok_rows // 2
    q_width = q_ref.shape[1] // (seq_count // 2)
    lanes = lax.broadcasted_iota(jnp.int32, (1, 128), 1)
    row = jnp.zeros((1, 128), jnp.float32)
    for t in range(tok_rows):
        pos = p_ref[0, t]
        row = jnp.where(lanes == 2 * t, (pos // code_base).astype(jnp.float32), row)
        row = jnp.where(lanes == 2 * t + 1, (pos % code_base).astype(jnp.float32), row)
    row = row.astype(o_ref.dtype)
    zeros = jnp.zeros((1, 128), o_ref.dtype)
    for s in range(seq_count):
        group, pair, head = s // 2, s % 2, s // (seq_count // KVH)
        for h in range(2):
            for j in range(half):
                t = h * half + j
                o_ref[s, h : h + 1, j * q_width : (j + 1) * q_width] = q_ref[t : t + 1, group * q_width : (group + 1) * q_width]
            k = pair * half + h
            base = half * q_width
            o_ref[s, h : h + 1, base : base + HD] = k_ref[k : k + 1, head * HD : (head + 1) * HD]
            o_ref[s, h : h + 1, base + HD : base + 2 * HD] = v_ref[k : k + 1, head * HD : (head + 1) * HD]
            o_ref[s, h : h + 1, base + 2 * HD :] = row if h == 0 else zeros


def build_send(queries, new_keys, new_values, positions, seq_count):
    tok_rows = queries.shape[0]
    width = (tok_rows // 2) * (queries.shape[1] // (seq_count // 2)) + 2 * HD + 128
    return pl.pallas_call(
        send_kernel,
        in_specs=[pl.BlockSpec(memory_space=pltpu.VMEM)] * 3 + [pl.BlockSpec(memory_space=pltpu.SMEM)],
        out_specs=pl.BlockSpec(memory_space=pltpu.VMEM),
        out_shape=jax.ShapeDtypeStruct((seq_count, 2, width), queries.dtype),
    )(queries, new_keys, new_values, positions.reshape(1, -1))


def on_device(queries, new_keys, new_values, positions, cache_keys, cache_values, slab_start):
    seq_count = lax.axis_size("seq")
    cell_axes = ("row", "col")
    row_count = lax.axis_size("row")
    col_count = lax.axis_size("col")
    cell_count = row_count * col_count
    heads_dev = HQ // seq_count
    group_size = HQ // KVH
    tok_rows = queries.shape[0]
    first_pos = slab_start[0]
    seq_index = lax.axis_index("seq")
    kv_first = seq_index * heads_dev // group_size
    parity = seq_index % 2
    core = lax.axis_index("row") % 2
    quarter = parity * 2 + core
    core_pairs = [(r, r ^ 1) for r in range(row_count)]
    seq_pairs = [(q, q ^ 1) for q in range(seq_count)]
    diag_pairs = [(q * row_count + r, (q ^ 1) * row_count + (r ^ 1)) for q in range(seq_count) for r in range(row_count)]
    width = 2 * HD
    pair_heads = 2 * heads_dev
    half_tok = tok_rows // 2

    send = build_send(queries, new_keys, new_values, positions, seq_count)
    recv = lax.all_to_all(send, "seq", 0, 0, tiled=True)
    q_half = half_tok * pair_heads * HD
    slab_rows = seq_count * tok_rows
    query_block = recv[:, :, :q_half].reshape(slab_rows, pair_heads, HD)
    slab_kv = recv[:, :, q_half : q_half + width].reshape(seq_count * half_tok, width)
    got_codes = recv[:, 0, q_half + width : q_half + width + tok_rows * 2].reshape(seq_count, tok_rows, 2)
    own_pos = decode(got_codes.reshape(slab_rows, 2))
    slab_codes = lax.dynamic_slice_in_dim(got_codes, parity * half_tok, half_tok, 1).reshape(seq_count * half_tok, 2)

    partner_q = swap(
        jnp.concatenate([query_block.reshape(slab_rows, -1), got_codes.reshape(slab_rows, 2)], axis=1), "row", core_pairs
    )
    partner_block = partner_q[:, : pair_heads * HD].reshape(slab_rows, pair_heads, HD)
    partner_pos = decode(partner_q[:, pair_heads * HD :])

    cache_block = jnp.concatenate(
        [
            lax.dynamic_slice_in_dim(cache_keys, kv_first * HD, HD, 1),
            lax.dynamic_slice_in_dim(cache_values, kv_first * HD, HD, 1),
        ],
        axis=1,
    )
    cache_len = cache_block.shape[0]
    part_cache = cache_len // 4
    half_slab = slab_kv.shape[0] // 2
    code_rows = jnp.pad(slab_codes.reshape(2, half_slab * 2), ((0, 0), (0, width - half_slab * 2)))
    cache_pair = lax.dynamic_slice_in_dim(cache_block, parity * 2 * part_cache, 2 * part_cache, 0)
    halves = jnp.stack(
        [
            jnp.concatenate(
                [
                    cache_pair[b * part_cache : (b + 1) * part_cache],
                    slab_kv[b * half_slab : (b + 1) * half_slab],
                    code_rows[b : b + 1],
                ],
                axis=0,
            )
            for b in range(2)
        ]
    )
    chunk_rows = halves.shape[1] * width // 128
    halves = halves.reshape(2, chunk_rows, 128)
    per_dest = jnp.broadcast_to(
        halves[None, :, None], (row_count // 2, 2, col_count) + halves.shape[1:]
    ).reshape((cell_count,) + halves.shape[1:])
    every = lax.all_to_all(per_dest, cell_axes, 0, 0, tiled=True)
    every = every.reshape(cell_count, -1, width)
    cache_got = every[:, :part_cache].reshape(-1, width)
    slab_got = every[:, part_cache : part_cache + half_slab].reshape(-1, width)
    key_pos_slab = decode(every[:, part_cache + half_slab, : 2 * half_slab].reshape(-1, 2))
    key_pos_cache = (
        jnp.arange(cell_count, dtype=jnp.int32)[:, None] * cache_len
        + quarter * part_cache
        + jnp.arange(part_cache, dtype=jnp.int32)[None, :]
    ).reshape(-1)
    keys = jnp.concatenate([cache_got[:, :HD], slab_got[:, :HD]], axis=0)
    values = jnp.concatenate([cache_got[:, HD:], slab_got[:, HD:]], axis=0)

    cache_count = cache_got.shape[0]
    their_max, their_sum, their_summed = partial_attention(
        partner_block, partner_pos, keys, values, key_pos_cache, key_pos_slab, cache_count, first_pos
    )
    theirs = jnp.concatenate([their_summed.reshape(slab_rows, -1), their_max, their_sum], axis=1)
    got = swap(theirs, "row", core_pairs)
    mine_max, mine_sum, mine_summed = partial_attention(
        query_block, own_pos, keys, values, key_pos_cache, key_pos_slab, cache_count, first_pos
    )

    split_at = pair_heads * HD
    other_summed = got[:, :split_at].reshape(slab_rows, pair_heads, HD)
    other_max = got[:, split_at : split_at + pair_heads]
    other_sum = got[:, split_at + pair_heads :]
    top = jnp.maximum(mine_max, other_max)
    scale_mine = jnp.exp(mine_max - top)
    scale_other = jnp.exp(other_max - top)
    numerator = mine_summed * scale_mine[..., None] + other_summed * scale_other[..., None]
    denominator = mine_sum * scale_mine + other_sum * scale_other
    normed = (numerator / denominator[..., None]).astype(jnp.bfloat16).reshape(slab_rows, -1)
    log_weight = top + jnp.log(denominator)
    pieces = []
    rest = log_weight
    for _ in range(3):
        piece = lax.reduce_precision(rest, exponent_bits=8, mantissa_bits=7)
        pieces.append(piece.astype(jnp.bfloat16))
        rest = rest - piece
    coded = jnp.stack(pieces, axis=1).reshape(slab_rows, -1)
    code_width = 128 * pl_cdiv(coded.shape[1], 128)
    coded = jnp.pad(coded, ((0, 0), (0, code_width - coded.shape[1])))
    partial = jnp.concatenate([normed, coded], axis=1)

    back = lax.all_to_all(partial.reshape(seq_count, tok_rows, -1), "seq", 0, 2, tiled=True)
    back = back.reshape(tok_rows, seq_count // 2, 2, -1)
    half_num = back[..., :split_at].astype(jnp.float32).reshape(tok_rows, seq_count // 2, 2, pair_heads, HD)
    half_log = (
        back[..., split_at : split_at + 3 * pair_heads]
        .astype(jnp.float32)
        .reshape(tok_rows, seq_count // 2, 2, 3, pair_heads)
        .sum(axis=3)
    )
    best = jnp.maximum(half_log[:, :, 0], half_log[:, :, 1])
    w0 = jnp.exp(half_log[:, :, 0] - best)
    w1 = jnp.exp(half_log[:, :, 1] - best)
    num = half_num[:, :, 0] * w0[..., None] + half_num[:, :, 1] * w1[..., None]
    context = (num / (w0 + w1)[..., None]).astype(jnp.bfloat16)
    return context.reshape(tok_rows, -1)


def pl_cdiv(a, b):
    return (a + b - 1) // b


def pl_heads(pair, heads_dev):
    return pair * heads_dev


def solution(mesh):
    in_specs = (
        P(("seq", "row", "col"), None),
        P(("seq", "row", "col"), None),
        P(("seq", "row", "col"), None),
        P(("seq", "row", "col")),
        P(("row", "col"), None),
        P(("row", "col"), None),
        P(),
    )
    out_specs = P(("seq", "row", "col"), None)
    return jax.shard_map(
        on_device, mesh=mesh, in_specs=in_specs, out_specs=out_specs, check_vma=False
    )
```
